32 devices in a mesh: group: 2 (over y), head: 4 (over z), req: 4 (over x, core).
Axes of the slice: x: 2, y: 2, z: 4, core: 2. Of those that a mesh axis runs over, the one named last changes fastest.
Arguments:
- x_input: bfloat16 [128, 8, 16384], P(('group', 'req'), None, 'head'), parts along dimension 0, may hold values from -6 to 6
- z_input: bfloat16 [128, 8, 16384], P(('group', 'req'), None, 'head'), parts along dimension 0, may hold values from -6 to 6
- bc_input: bfloat16 [128, 8, 4096], P(('group', 'req')), parts along dimension 0, may hold values from -6 to 6
- dt_input: float32 [128, 8, 256], P(('group', 'req'), None, 'head'), parts along dimension 0, may hold values from -6 to 6
- conv_x_state: bfloat16 [128, 3, 16384], P(('group', 'req'), None, 'head'), parts along dimension 0, may hold values from -6 to 6
- conv_bc_state: bfloat16 [128, 3, 4096], P(('group', 'req')), parts along dimension 0, may hold values from -6 to 6
- ssm_state: bfloat16 [128, 256, 64, 256], P(('group', 'req'), 'head'), parts along dimension 0, may hold values from -6 to 6
- accepted: int32 [128], P(('group', 'req')), parts along dimension 0, may hold values from 0 to 8
- next_owner: int32 [128], P('group'), parts along dimension 0, may hold values from 0 to 3, as said below
- conv_x_weight: float32 [4, 16384], P(None, 'head'), may hold values from -3 to 3
- conv_x_bias: float32 [16384], P('head'), may hold values from -3 to 3
- conv_bc_weight: float32 [4, 4096], replicated, may hold values from -3 to 3
- conv_bc_bias: float32 [4096], replicated, may hold values from -3 to 3
- dt_bias: float32 [256], P('head'), may hold values from -3 to 0
- a_log: float32 [256], P('head'), may hold values from -4 to 1
- d_skip: float32 [256], P('head'), may hold values from 0.5 to 1.5
- norm_gain: float32 [16384], P('head'), may hold values from 0.5 to 1.5
- out_weight: bfloat16 [16384, 8192], P('head'), may hold values from -0.0625 to 0.0625
Outputs:
- mixed: bfloat16 [128, 8, 8192], P(('group', 'req'), None, 'head'), parts along dimension 0
- new_ssm_state: bfloat16 [128, 256, 64, 256], P(('group', 'req'), 'head'), parts along dimension 0
- new_conv_x_state: bfloat16 [128, 3, 16384], P(('group', 'req'), None, 'head'), parts along dimension 0
- new_conv_bc_state: bfloat16 [128, 3, 4096], P(('group', 'req')), parts along dimension 0
The draws below stay inside these ranges and needn't reach their ends.
There are 2 independent parts, one for each index of `group`. The reference program is written for one: setup_inputs(seed, part) draws one part's arguments, and reference() takes and returns one part's arrays. A program takes and returns all parts, laid end to end along the dimension named above; an argument that names none is the same for every part. Nothing has to cross between parts.
Inputs may be any that keep to these rules, and one draw needn't show every extreme that they name: Every index of req is next_owner of exactly 16 requests, and at most 8 of the requests of one index of req (requests i * 16 .. i * 16 + 15) share one next_owner.
All inputs are finite; a program needn't handle non-finite values.
Results may differ from the reference program's by a relative error of at most 0.0049.
Values may be sent and summed in bfloat16 or wider, within the bound.
No kernel may reach another device: no remote copies, remote signals or barrier semaphores. Data moves between devices by JAX's collectives and lax.ppermute only.
A program may use at most 576 MiB of HBM per device.

```python
import jax
import jax.numpy as jnp
from jax import lax

D = 8192
H = 256
P_SIZE = 64
N = 256
G = 8
K = 4
L = 8
REQ_DEV = 16
R = 64
CAP = 8
N_REQ = 4


def draw_next_owner(key, part):
    rotation_key, order_key = jax.random.split(key)
    rotation = jax.random.randint(rotation_key, (), 0, N_REQ)
    remainder = REQ_DEV - CAP
    places = jnp.arange(REQ_DEV, dtype=jnp.int32) - CAP
    steps_up = jnp.arange(1, N_REQ, dtype=jnp.int32) * remainder // (N_REQ - 1)
    offsets = jnp.where(places < 0, 0, 1 + jnp.sum((steps_up[None, :] <= places[:, None]).astype(jnp.int32), axis=1))
    sources = jnp.arange(N_REQ, dtype=jnp.int32)
    assigned = (sources[:, None] + rotation + offsets[None, :]) % N_REQ
    block_keys = jax.random.split(order_key, N_REQ)
    orders = jax.vmap(lambda one_key: jax.random.permutation(one_key, REQ_DEV))(block_keys)
    shuffled = jnp.take_along_axis(assigned, orders.astype(jnp.int32), axis=1)
    return shuffled.reshape(N_REQ * REQ_DEV).astype(jnp.int32)


def place_ends(drawn, key, least, top_value):
    extent = drawn.shape
    place = [jax.random.randint(jax.random.fold_in(key, axis), (), 0, extent[axis]) for axis in range(len(extent))]
    drawn = drawn.at[tuple(place)].set(least)
    longest = extent.index(max(extent))
    place[longest] = (place[longest] + 1) % extent[longest]
    return drawn.at[tuple(place)].set(top_value)


def strengthened(array, key, source, target, shards_of, factor):
    owner, partner = [(jnp.arange(array.shape[dim]) // (array.shape[dim] // shards_of)).reshape([-1 if axis == dim else 1 for axis in range(array.ndim)]) for dim in (source, target)]
    chosen = jax.random.permutation(key, shards_of)[partner]
    strong = (owner == chosen) | (owner == (partner + shards_of // 2) % shards_of)
    return jnp.where(strong, factor * array, array)


def block_scale(key, dims, cuts, smallest, high):
    factor_of, own = 1.0, jax.random.fold_in(key, 6)
    for axis_at, parts in cuts:
        draws = jnp.exp(jax.random.uniform(jax.random.fold_in(own, axis_at), (parts,), jnp.float32, smallest / len(cuts), high / len(cuts)))
        factor_of = factor_of * jnp.repeat(draws, dims[axis_at] // parts).reshape([-1 if axis == axis_at else 1 for axis in range(len(dims))])
    return factor_of


def centred(key, shape, width, most, shards=(), kind=jnp.bfloat16):
    values = jax.random.normal(key, shape, jnp.float32) * width
    if len(shards) > 0:
        values = block_scale(key, shape, shards, -0.22, 0.18) * values
    return jnp.clip(values, min=-most, max=most).astype(kind)


def noise_with(stream_key, extent, spread, bound, pieces, heavy, held_as=jnp.bfloat16):
    drawn = spread * jax.random.normal(stream_key, extent, jnp.float32)
    if pieces:
        drawn = drawn * block_scale(stream_key, extent, pieces, -0.22, 0.18)
    return jnp.clip(strengthened(drawn, jax.random.fold_in(stream_key, 3), *heavy), -bound, bound).astype(held_as)


def setup_inputs(seed: int = 0, part: int = 0) -> dict:
    keys = jax.random.split(jax.random.key(seed), 19)
    part_keys = jax.random.split(jax.random.fold_in(keys[18], part), 19)
    x_input = centred(part_keys[0], (R, L, H * P_SIZE), 1.0, 6.0, ((0, 4), (2, 4)))
    z_input = centred(part_keys[1], (R, L, H * P_SIZE), 1.0, 6.0, ((0, 4), (2, 4)))
    bc_input = centred(part_keys[2], (R, L, 2 * G * N), 1.0, 6.0, ((0, 4),))
    dt_input = centred(part_keys[3], (R, L, H), 1.0, 6.0, ((0, 4), (2, 4)), jnp.float32)
    conv_x_state = centred(part_keys[4], (R, K - 1, H * P_SIZE), 1.0, 6.0, ((0, 4), (2, 4)))
    conv_bc_state = centred(part_keys[5], (R, K - 1, 2 * G * N), 1.0, 6.0, ((0, 4),))
    ssm_state = centred(part_keys[6], (R, H, P_SIZE, N), 1.0, 6.0, ((0, 4), (1, 4)))
    accepted = place_ends(jax.random.randint(part_keys[7], (R,), 0, L + 1), jax.random.fold_in(part_keys[7], 1), 0, L).astype(jnp.int32)
    next_owner = draw_next_owner(jax.random.fold_in(jax.random.fold_in(keys[18], part), 71), part)
    conv_x_weight = centred(keys[9], (K, H * P_SIZE), K ** -0.5, 3.0, ((1, 4),), jnp.float32)
    conv_x_bias = centred(keys[10], (H * P_SIZE,), 0.5, 3.0, ((0, 4),), jnp.float32)
    conv_bc_weight = centred(keys[11], (K, 2 * G * N), K ** -0.5, 3.0, (), jnp.float32)
    conv_bc_bias = centred(keys[12], (2 * G * N,), 0.5, 3.0, (), jnp.float32)
    dt_bias = jnp.clip(-3.0 + 3.0 * jax.random.uniform(keys[13], (H,), jnp.float32) ** block_scale(keys[13], (H,), ((0, 4),), -0.2, 0.2), -3.0, 0.0)
    a_log = jnp.clip(-4.0 + 5.0 * jax.random.uniform(keys[14], (H,), jnp.float32) ** block_scale(keys[14], (H,), ((0, 4),), -0.2, 0.2), -4.0, 1.0)
    d_skip = jnp.clip(0.5 + 1.0 * jax.random.uniform(keys[15], (H,), jnp.float32) ** block_scale(keys[15], (H,), ((0, 4),), -0.2, 0.2), 0.5, 1.5)
    norm_gain = jnp.clip(0.5 + 1.0 * jax.random.uniform(keys[16], (H * P_SIZE,), jnp.float32) ** block_scale(keys[16], (H * P_SIZE,), ((0, 4),), -0.2, 0.2), 0.5, 1.5)
    out_weight = noise_with(keys[17], (H * P_SIZE, D), (H * P_SIZE) ** -0.5, 0.0625, ((0, 4),), (0, 1, 4, 2.0))
    return dict(x_input=x_input, z_input=z_input, bc_input=bc_input, dt_input=dt_input, conv_x_state=conv_x_state, conv_bc_state=conv_bc_state, ssm_state=ssm_state, accepted=accepted, next_owner=next_owner, conv_x_weight=conv_x_weight, conv_x_bias=conv_x_bias, conv_bc_weight=conv_bc_weight, conv_bc_bias=conv_bc_bias, dt_bias=dt_bias, a_log=a_log, d_skip=d_skip, norm_gain=norm_gain, out_weight=out_weight)


epsilon = 1e-05

def conv_window(history, inputs, weight, bias_vector):
    joined = jnp.concatenate([history, inputs], axis=1)
    widened = joined.astype(jnp.float32)
    accumulated = bias_vector[None, None, :] + weight[0][None, None, :] * widened[:, 0:L, :]
    for offset in range(1, K):
        accumulated = accumulated + weight[offset][None, None, :] * widened[:, offset:offset + L, :]
    return (jax.nn.silu(accumulated), joined)

def keep_rows(joined, accepted):
    row_index = accepted[:, None].astype(jnp.int32) + jnp.arange(K - 1, dtype=jnp.int32)[None, :]
    return jnp.take_along_axis(joined, row_index[:, :, None], axis=1)

def scan_request(arguments):
    initial, x_heads, b_heads, c_heads, decay_rate, step_size, accepted_one = arguments

    def advance(carried, inputs):
        current, retained = carried
        x_now, b_now, c_now, decay_now, step_now, moment = inputs
        current = decay_now[:, None, None] * current + (step_now[:, None] * x_now)[:, :, None] * b_now[:, None, :]
        reading = lax.optimization_barrier(jnp.sum(current * c_now[:, None, :], axis=2))
        retained = jnp.where(moment + 1 == accepted_one, current, retained)
        return ((current, retained), reading)
    positions = jnp.arange(L, dtype=jnp.int32)
    (final_state, retained), readings = lax.scan(advance, (initial, initial), (x_heads, b_heads, c_heads, decay_rate, step_size, positions))
    return (readings, retained)

def reference(x_input, z_input, bc_input, dt_input, conv_x_state, conv_bc_state, ssm_state, accepted, next_owner, conv_x_weight, conv_x_bias, conv_bc_weight, conv_bc_bias, dt_bias, a_log, d_skip, norm_gain, out_weight):
    x_conv, x_joined = conv_window(conv_x_state, x_input, conv_x_weight, conv_x_bias)
    bc_conv, bc_joined = conv_window(conv_bc_state, bc_input, conv_bc_weight, conv_bc_bias)
    requests = x_input.shape[0]
    heads_group = H // G
    step_size = jax.nn.softplus(dt_input + dt_bias[None, None, :])
    decay_rate = jnp.exp(-jnp.exp(a_log)[None, None, :] * step_size)
    x_heads = x_conv.reshape(requests, L, H, P_SIZE)
    b_heads = jnp.repeat(bc_conv[:, :, :G * N].reshape(requests, L, G, N), heads_group, axis=2)
    c_heads = jnp.repeat(bc_conv[:, :, G * N:].reshape(requests, L, G, N), heads_group, axis=2)
    readings, retained = lax.map(scan_request, (ssm_state.astype(jnp.float32), x_heads, b_heads, c_heads, decay_rate, step_size, accepted))
    y_values = readings + d_skip[None, None, :, None] * x_heads
    gated = y_values.reshape(requests, L, H * P_SIZE) * jax.nn.silu(z_input.astype(jnp.float32))
    grouped = gated.reshape(requests, L, H, P_SIZE)
    inverse_rms = lax.rsqrt(lax.optimization_barrier(jnp.mean(grouped * grouped, axis=3, keepdims=True)) + epsilon)
    normed = ((grouped * inverse_rms).reshape(requests, L, H * P_SIZE) * norm_gain[None, None, :]).astype(jnp.bfloat16)
    mixed = jnp.dot(normed.reshape(requests * L, H * P_SIZE), out_weight, preferred_element_type=jnp.float32)
    mixed = mixed.astype(jnp.bfloat16).reshape(requests, L, D)
    arrival = jnp.argsort(next_owner, stable=True).astype(jnp.int32)
    new_ssm_state = retained.astype(jnp.bfloat16)[arrival]
    new_conv_x_state = keep_rows(x_joined, accepted)[arrival]
    new_conv_bc_state = keep_rows(bc_joined, accepted)[arrival]
    return (mixed, new_ssm_state, new_conv_x_state, new_conv_bc_state)
```

```python
import jax
import jax.numpy as jnp
from jax import lax
from jax.sharding import PartitionSpec as P

D = 8192
H = 256
P_SIZE = 64
N = 256
G = 8
K = 4
L = 8
CAP = 8


epsilon = 1e-05
highest = lax.Precision.HIGHEST


def conv_window(history, inputs, weight, bias_vector):
    joined = jnp.concatenate([history, inputs], axis=1)
    widened = joined.astype(jnp.float32)
    accumulated = bias_vector[None, None, :] + weight[0][None, None, :] * widened[:, 0:L, :]
    for offset in range(1, K):
        accumulated = (
            accumulated + weight[offset][None, None, :] * widened[:, offset : offset + L, :]
        )
    return (jax.nn.silu(accumulated), joined)


def on_device(
    x_input,
    z_input,
    bc_input,
    dt_input,
    conv_x_state,
    conv_bc_state,
    ssm_state,
    accepted,
    next_owner,
    conv_x_weight,
    conv_x_bias,
    conv_bc_weight,
    conv_bc_bias,
    dt_bias,
    a_log,
    d_skip,
    norm_gain,
    out_weight,
):
    local_requests = x_input.shape[0]
    local_heads = dt_input.shape[2]
    head_index = lax.axis_index("head")
    req_index = lax.axis_index("req")
    all_requests = next_owner.shape[0]
    heads_group = H // G
    x_conv, x_joined = conv_window(conv_x_state, x_input, conv_x_weight, conv_x_bias)
    bc_conv, bc_joined = conv_window(conv_bc_state, bc_input, conv_bc_weight, conv_bc_bias)
    step_size = jax.nn.softplus(dt_input + dt_bias[None, None, :])
    log_decay = -jnp.exp(a_log)[None, None, :] * step_size
    global_heads = head_index * local_heads + jnp.arange(local_heads, dtype=jnp.int32)
    group_pick = (
        global_heads[:, None] // heads_group == jnp.arange(G, dtype=jnp.int32)[None, :]
    ).astype(jnp.float32)
    b_groups = bc_conv[:, :, : G * N].reshape(local_requests, L, G, N)
    c_groups = bc_conv[:, :, G * N :].reshape(local_requests, L, G, N)
    b_heads = jnp.einsum("rlgn,hg->rlhn", b_groups, group_pick, precision=highest)
    c_heads = jnp.einsum("rlgn,hg->rlhn", c_groups, group_pick, precision=highest)
    x_heads = x_conv.reshape(local_requests, L, local_heads, P_SIZE)
    initial = ssm_state.astype(jnp.float32)
    inclusive = jnp.cumsum(log_decay, axis=1)
    before = jnp.concatenate(
        [jnp.zeros((local_requests, 1, local_heads), jnp.float32), inclusive], axis=1
    )
    positions = jnp.arange(L, dtype=jnp.int32)
    causal = positions[:, None] >= positions[None, :]
    by_head = inclusive.transpose(0, 2, 1)
    differences = by_head[:, :, :, None] - by_head[:, :, None, :]
    pair_decay = jnp.exp(jnp.where(causal[None, None], differences, -jnp.inf))
    scores = jnp.einsum("rthn,rshn->rhts", c_heads, b_heads, precision=highest)
    weights = scores * pair_decay * step_size.transpose(0, 2, 1)[:, :, None, :]
    within = jnp.einsum("rhts,rshp->rthp", weights, x_heads, precision=highest)
    carried = jnp.exp(inclusive)[:, :, :, None] * jnp.einsum(
        "rhpn,rthn->rthp", initial, c_heads, precision=highest
    )
    y_values = within + carried + d_skip[None, None, :, None] * x_heads
    count_pick = (jnp.arange(L + 1, dtype=jnp.int32)[None, :] == accepted[:, None]).astype(
        jnp.float32
    )
    reached = jnp.einsum("ra,rah->rh", count_pick, before, precision=highest)
    valid = positions[None, :] < accepted[:, None]
    exponent = jnp.where(valid[:, :, None], reached[:, None, :] - inclusive, -jnp.inf)
    token_weight = jnp.exp(exponent) * step_size
    retained = jnp.exp(reached)[:, :, None, None] * initial + jnp.einsum(
        "rsh,rshp,rshn->rhpn", token_weight, x_heads, b_heads, precision=highest
    )
    retained = retained.astype(jnp.bfloat16)
    gated = y_values.reshape(local_requests, L, local_heads * P_SIZE) * jax.nn.silu(
        z_input.astype(jnp.float32)
    )
    blocks = gated.reshape(local_requests, L, local_heads, P_SIZE)
    inverse_rms = lax.rsqrt(jnp.mean(blocks * blocks, axis=3, keepdims=True) + epsilon)
    normed = (
        (blocks * inverse_rms).reshape(local_requests, L, local_heads * P_SIZE)
        * norm_gain[None, None, :]
    ).astype(jnp.bfloat16)
    partial_terms = jnp.dot(
        normed.reshape(local_requests * L, local_heads * P_SIZE),
        out_weight,
        preferred_element_type=jnp.float32,
    )
    share_width = D // lax.axis_size("head")
    share = lax.psum_scatter(partial_terms, "head", scatter_dimension=1, tiled=True)
    mixed = share.astype(jnp.bfloat16).reshape(local_requests, L, share_width)
    window_rows = jnp.arange(K - 1 + L, dtype=jnp.int32)
    row_pick = (
        window_rows[None, None, :]
        == accepted[:, None, None] + jnp.arange(K - 1, dtype=jnp.int32)[None, :, None]
    ).astype(jnp.bfloat16)
    kept_x = jnp.einsum(
        "rkt,rtc->rkc", row_pick, x_joined, preferred_element_type=jnp.float32
    ).astype(jnp.bfloat16)
    kept_bc = jnp.einsum(
        "rkt,rtc->rkc", row_pick, bc_joined, preferred_element_type=jnp.float32
    ).astype(jnp.bfloat16)
    requests_per_owner = local_requests
    owners = lax.axis_size("req")
    cap = min(CAP, local_requests)
    request_ids = jnp.arange(all_requests, dtype=jnp.int32)
    source = request_ids // requests_per_owner
    same_owner = next_owner[:, None] == next_owner[None, :]
    earlier = request_ids[None, :] < request_ids[:, None]
    rank_at_owner = jnp.sum((same_owner & earlier).astype(jnp.int32), axis=1)
    same_source = source[:, None] == source[None, :]
    rank_in_pair = jnp.sum((same_owner & earlier & same_source).astype(jnp.int32), axis=1)
    local_owner = lax.dynamic_slice_in_dim(next_owner, req_index * local_requests, local_requests)
    local_rank = lax.dynamic_slice_in_dim(rank_in_pair, req_index * local_requests, local_requests)
    slot_rows = jnp.arange(local_requests, dtype=jnp.int32)
    chosen = (local_owner[None, None, :] == jnp.arange(owners, dtype=jnp.int32)[:, None, None]) & (
        local_rank[None, None, :] == jnp.arange(cap, dtype=jnp.int32)[None, :, None]
    )
    send_index = jnp.sum(jnp.where(chosen, slot_rows[None, None, :], 0), axis=2).reshape(-1)
    arriving = (next_owner[None, :] == req_index) & (rank_at_owner[None, :] == slot_rows[:, None])
    receive_index = jnp.sum(
        jnp.where(arriving, source[None, :] * cap + rank_in_pair[None, :], 0), axis=1
    )

    def hand_over(values):
        outgoing = jnp.take(values, send_index, axis=0, mode="clip")
        incoming = lax.all_to_all(outgoing, "req", 0, 0, tiled=True)
        return jnp.take(incoming, receive_index, axis=0, mode="clip")

    new_ssm_state = hand_over(retained)
    new_conv_x_state = hand_over(kept_x)
    new_conv_bc_state = hand_over(kept_bc)
    return (mixed, new_ssm_state, new_conv_x_state, new_conv_bc_state)


def solution(mesh):
    placed = (
        P(("group", "req"), None, "head"),
        P(("group", "req"), None, "head"),
        P(("group", "req"), None, None),
        P(("group", "req"), None, "head"),
        P(("group", "req"), None, "head"),
        P(("group", "req"), None, None),
        P(("group", "req"), "head", None, None),
        P(("group", "req")),
        P("group"),
        P(None, "head"),
        P("head"),
        P(),
        P(),
        P("head"),
        P("head"),
        P("head"),
        P("head"),
        P("head", None),
    )
    return jax.shard_map(
        on_device,
        mesh=mesh,
        in_specs=placed,
        out_specs=(
            P(("group", "req"), None, "head"),
            P(("group", "req"), "head", None, None),
            P(("group", "req"), None, "head"),
            P(("group", "req"), None, None),
        ),
        check_vma=False,
    )
```

```python
import jax
import jax.numpy as jnp
from jax import lax
from jax.sharding import PartitionSpec as P
from jax.experimental import pallas as pl
from jax.experimental.pallas import tpu as pltpu

D = 8192
H = 256
P_SIZE = 64
N = 256
G = 8
K = 4
L = 8
CAP = 8


epsilon = 1e-05
highest = lax.Precision.HIGH


def conv_window(history, inputs, weight, bias_vector):
    joined = jnp.concatenate([history, inputs], axis=1)
    widened = joined.astype(jnp.float32)
    accumulated = bias_vector[None, None, :] + weight[0][None, None, :] * widened[:, 0:L, :]
    for offset in range(1, K):
        accumulated = (
            accumulated + weight[offset][None, None, :] * widened[:, offset : offset + L, :]
        )
    return (jax.nn.silu(accumulated), joined)


def assemble(piece_of, slot_of, pieces):
    rows = piece_of.shape[0]
    count = len(pieces)

    def kernel(piece_ref, slot_ref, *refs):
        sources = refs[:count]
        out_ref = refs[count]
        sem = refs[count + 1]

        def start(row, carry):
            piece = piece_ref[row]
            slot = slot_ref[row]
            for which, ref in enumerate(sources):

                @pl.when(piece == which)
                def _():
                    pltpu.make_async_copy(ref.at[slot], out_ref.at[row], sem.at[row]).start()

            return carry

        lax.fori_loop(0, rows, start, 0)

        def finish(row, carry):
            pltpu.make_async_copy(sources[0].at[0], out_ref.at[row], sem.at[row]).wait()
            return carry

        lax.fori_loop(0, rows, finish, 0)

    smem = pl.BlockSpec(memory_space=pltpu.SMEM)
    anywhere = pl.BlockSpec(memory_space=pl.ANY)
    return pl.pallas_call(
        kernel,
        out_shape=jax.ShapeDtypeStruct((rows,) + pieces[0].shape[1:], pieces[0].dtype),
        in_specs=[smem, smem] + [anywhere] * count,
        out_specs=anywhere,
        scratch_shapes=[pltpu.SemaphoreType.DMA((rows,))],
    )(piece_of, slot_of, *pieces)


def on_device(
    x_input,
    z_input,
    bc_input,
    dt_input,
    conv_x_state,
    conv_bc_state,
    ssm_state,
    accepted,
    next_owner,
    conv_x_weight,
    conv_x_bias,
    conv_bc_weight,
    conv_bc_bias,
    dt_bias,
    a_log,
    d_skip,
    norm_gain,
    out_weight,
):
    local_requests = x_input.shape[0]
    local_heads = dt_input.shape[2]
    head_index = lax.axis_index("head")
    req_index = lax.axis_index("req")
    all_requests = next_owner.shape[0]
    heads_group = H // G
    x_conv, x_joined = conv_window(conv_x_state, x_input, conv_x_weight, conv_x_bias)
    bc_conv, bc_joined = conv_window(conv_bc_state, bc_input, conv_bc_weight, conv_bc_bias)
    step_size = jax.nn.softplus(dt_input + dt_bias[None, None, :])
    log_decay = -jnp.exp(a_log)[None, None, :] * step_size
    global_heads = head_index * local_heads + jnp.arange(local_heads, dtype=jnp.int32)
    group_pick = (
        global_heads[:, None] // heads_group == jnp.arange(G, dtype=jnp.int32)[None, :]
    ).astype(jnp.float32)
    b_groups = bc_conv[:, :, : G * N].reshape(local_requests, L, G, N)
    c_groups = bc_conv[:, :, G * N :].reshape(local_requests, L, G, N)
    b_heads = jnp.einsum("rlgn,hg->rlhn", b_groups, group_pick, precision=highest)
    c_heads = jnp.einsum("rlgn,hg->rlhn", c_groups, group_pick, precision=highest)
    x_heads = x_conv.reshape(local_requests, L, local_heads, P_SIZE)
    initial = ssm_state.astype(jnp.float32)
    inclusive = jnp.cumsum(log_decay, axis=1)
    before = jnp.concatenate(
        [jnp.zeros((local_requests, 1, local_heads), jnp.float32), inclusive], axis=1
    )
    positions = jnp.arange(L, dtype=jnp.int32)
    causal = positions[:, None] >= positions[None, :]
    by_head = inclusive.transpose(0, 2, 1)
    differences = by_head[:, :, :, None] - by_head[:, :, None, :]
    pair_decay = jnp.exp(jnp.where(causal[None, None], differences, -jnp.inf))
    scores = jnp.einsum("rthn,rshn->rhts", c_heads, b_heads, precision=highest)
    weights = scores * pair_decay * step_size.transpose(0, 2, 1)[:, :, None, :]
    within = jnp.einsum("rhts,rshp->rthp", weights, x_heads, precision=highest)
    carried = jnp.exp(inclusive)[:, :, :, None] * jnp.einsum(
        "rhpn,rthn->rthp", initial, c_heads, precision=highest
    )
    y_values = within + carried + d_skip[None, None, :, None] * x_heads
    count_pick = (jnp.arange(L + 1, dtype=jnp.int32)[None, :] == accepted[:, None]).astype(
        jnp.float32
    )
    reached = jnp.einsum("ra,rah->rh", count_pick, before, precision=highest)
    valid = positions[None, :] < accepted[:, None]
    exponent = jnp.where(valid[:, :, None], reached[:, None, :] - inclusive, -jnp.inf)
    token_weight = jnp.exp(exponent) * step_size
    weighted_x = token_weight[:, :, :, None] * x_heads
    retained = jnp.exp(reached)[:, :, None, None] * initial + jnp.einsum(
        "rshp,rshn->rhpn", weighted_x, b_heads, precision=highest
    )
    retained = retained.astype(jnp.bfloat16)
    gated = y_values.reshape(local_requests, L, local_heads * P_SIZE) * jax.nn.silu(
        z_input.astype(jnp.float32)
    )
    blocks = gated.reshape(local_requests, L, local_heads, P_SIZE)
    inverse_rms = lax.rsqrt(jnp.mean(blocks * blocks, axis=3, keepdims=True) + epsilon)
    normed = (
        (blocks * inverse_rms).reshape(local_requests, L, local_heads * P_SIZE)
        * norm_gain[None, None, :]
    ).astype(jnp.bfloat16)
    partial_terms = jnp.dot(
        normed.reshape(local_requests * L, local_heads * P_SIZE),
        out_weight,
        preferred_element_type=jnp.float32,
    )
    share_width = D // lax.axis_size("head")
    share = lax.psum_scatter(partial_terms, "head", scatter_dimension=1, tiled=True)
    mixed = share.astype(jnp.bfloat16).reshape(local_requests, L, share_width)
    window_rows = jnp.arange(K - 1 + L, dtype=jnp.int32)
    row_pick = (
        window_rows[None, None, :]
        == accepted[:, None, None] + jnp.arange(K - 1, dtype=jnp.int32)[None, :, None]
    ).astype(jnp.bfloat16)
    kept_x = jnp.einsum(
        "rkt,rtc->rkc", row_pick, x_joined, preferred_element_type=jnp.float32
    ).astype(jnp.bfloat16)
    kept_bc = jnp.einsum(
        "rkt,rtc->rkc", row_pick, bc_joined, preferred_element_type=jnp.float32
    ).astype(jnp.bfloat16)
    requests_per_owner = local_requests
    owners = lax.axis_size("req")
    cap = min(CAP, local_requests)
    request_ids = jnp.arange(all_requests, dtype=jnp.int32)
    source = request_ids // requests_per_owner
    same_owner = next_owner[:, None] == next_owner[None, :]
    earlier = request_ids[None, :] < request_ids[:, None]
    rank_at_owner = jnp.sum((same_owner & earlier).astype(jnp.int32), axis=1)
    same_source = source[:, None] == source[None, :]
    rank_in_pair = jnp.sum((same_owner & earlier & same_source).astype(jnp.int32), axis=1)
    local_owner = lax.dynamic_slice_in_dim(next_owner, req_index * local_requests, local_requests)
    local_rank = lax.dynamic_slice_in_dim(rank_in_pair, req_index * local_requests, local_requests)
    slot_rows = jnp.arange(local_requests, dtype=jnp.int32)
    chosen = (local_owner[None, None, :] == jnp.arange(owners, dtype=jnp.int32)[:, None, None]) & (
        local_rank[None, None, :] == jnp.arange(cap, dtype=jnp.int32)[None, :, None]
    )
    send_index = jnp.sum(jnp.where(chosen, slot_rows[None, None, :], 0), axis=2).reshape(-1)
    arriving = (next_owner[None, :] == req_index) & (rank_at_owner[None, :] == slot_rows[:, None])
    receive_index = jnp.sum(
        jnp.where(arriving, source[None, :] * cap + rank_in_pair[None, :], 0), axis=1
    )

    partner_bits = range(1, owners)
    own_index = jnp.take(send_index.reshape(owners, cap), req_index, axis=0)
    pair_index = [
        jnp.take(send_index.reshape(owners, cap), req_index ^ bits, axis=0) for bits in partner_bits
    ]
    arriving_source = jnp.sum(jnp.where(arriving, source[None, :], 0), axis=1)
    arriving_rank = jnp.sum(jnp.where(arriving, rank_in_pair[None, :], 0), axis=1)
    gather_index = (arriving_source ^ req_index) * cap + arriving_rank

    piece_of = jnp.clip(arriving_source ^ req_index, 0, owners - 1)
    slot_of = jnp.clip(arriving_rank, 0, cap - 1)

    def send_pieces(values):
        pieces = [jnp.take(values, own_index, axis=0, mode="clip")]
        for bits, index in zip(partner_bits, pair_index):
            outgoing = jnp.take(values, index, axis=0, mode="clip")
            pairs = [(i, i ^ bits) for i in range(owners)]
            pieces.append(lax.ppermute(outgoing, "req", pairs))
        return pieces

    def hand_over(values):
        pieces = send_pieces(values)
        return jnp.take(jnp.concatenate(pieces, axis=0), gather_index, axis=0, mode="clip")

    new_ssm_state = assemble(piece_of, slot_of, send_pieces(retained))
    new_conv_x_state = hand_over(kept_x)
    new_conv_bc_state = hand_over(kept_bc)
    return (mixed, new_ssm_state, new_conv_x_state, new_conv_bc_state)


def solution(mesh):
    placed = (
        P(("group", "req"), None, "head"),
        P(("group", "req"), None, "head"),
        P(("group", "req"), None, None),
        P(("group", "req"), None, "head"),
        P(("group", "req"), None, "head"),
        P(("group", "req"), None, None),
        P(("group", "req"), "head", None, None),
        P(("group", "req")),
        P("group"),
        P(None, "head"),
        P("head"),
        P(),
        P(),
        P("head"),
        P("head"),
        P("head"),
        P("head"),
        P("head", None),
    )
    return jax.shard_map(
        on_device,
        mesh=mesh,
        in_specs=placed,
        out_specs=(
            P(("group", "req"), None, "head"),
            P(("group", "req"), "head", None, None),
            P(("group", "req"), None, "head"),
            P(("group", "req"), None, None),
        ),
        check_vma=False,
    )
```

```python
import jax
import jax.numpy as jnp
from jax import lax
from jax.sharding import PartitionSpec as P

D = 8192
H = 256
P_SIZE = 64
N = 256
G = 8
K = 4
L = 8
CAP = 8


epsilon = 1e-05
highest = lax.Precision.HIGH


def conv_window(history, inputs, weight, bias_vector):
    joined = jnp.concatenate([history, inputs], axis=1)
    widened = joined.astype(jnp.float32)
    accumulated = bias_vector[None, None, :] + weight[0][None, None, :] * widened[:, 0:L, :]
    for offset in range(1, K):
        accumulated = (
            accumulated + weight[offset][None, None, :] * widened[:, offset : offset + L, :]
        )
    return (jax.nn.silu(accumulated), joined)


def on_device(
    x_input,
    z_input,
    bc_input,
    dt_input,
    conv_x_state,
    conv_bc_state,
    ssm_state,
    accepted,
    next_owner,
    conv_x_weight,
    conv_x_bias,
    conv_bc_weight,
    conv_bc_bias,
    dt_bias,
    a_log,
    d_skip,
    norm_gain,
    out_weight,
):
    local_requests = x_input.shape[0]
    local_heads = dt_input.shape[2]
    head_index = lax.axis_index("head")
    req_index = lax.axis_index("req")
    all_requests = next_owner.shape[0]
    heads_group = H // G
    x_conv, x_joined = conv_window(conv_x_state, x_input, conv_x_weight, conv_x_bias)
    bc_conv, bc_joined = conv_window(conv_bc_state, bc_input, conv_bc_weight, conv_bc_bias)
    step_size = jax.nn.softplus(dt_input + dt_bias[None, None, :])
    log_decay = -jnp.exp(a_log)[None, None, :] * step_size
    global_heads = head_index * local_heads + jnp.arange(local_heads, dtype=jnp.int32)
    group_pick = (
        global_heads[:, None] // heads_group == jnp.arange(G, dtype=jnp.int32)[None, :]
    ).astype(jnp.float32)
    b_groups = bc_conv[:, :, : G * N].reshape(local_requests, L, G, N)
    c_groups = bc_conv[:, :, G * N :].reshape(local_requests, L, G, N)
    b_heads = jnp.einsum("rlgn,hg->rlhn", b_groups, group_pick, precision=highest)
    c_heads = jnp.einsum("rlgn,hg->rlhn", c_groups, group_pick, precision=highest)
    x_heads = x_conv.reshape(local_requests, L, local_heads, P_SIZE)
    initial = ssm_state.astype(jnp.float32)
    inclusive = jnp.cumsum(log_decay, axis=1)
    before = jnp.concatenate(
        [jnp.zeros((local_requests, 1, local_heads), jnp.float32), inclusive], axis=1
    )
    positions = jnp.arange(L, dtype=jnp.int32)
    causal = positions[:, None] >= positions[None, :]
    by_head = inclusive.transpose(0, 2, 1)
    differences = by_head[:, :, :, None] - by_head[:, :, None, :]
    pair_decay = jnp.exp(jnp.where(causal[None, None], differences, -jnp.inf))
    scores = jnp.einsum("rthn,rshn->rhts", c_heads, b_heads, precision=highest)
    weights = scores * pair_decay * step_size.transpose(0, 2, 1)[:, :, None, :]
    within = jnp.einsum("rhts,rshp->rthp", weights, x_heads, precision=highest)
    carried = jnp.exp(inclusive)[:, :, :, None] * jnp.einsum(
        "rhpn,rthn->rthp", initial, c_heads, precision=highest
    )
    y_values = within + carried + d_skip[None, None, :, None] * x_heads
    count_pick = (jnp.arange(L + 1, dtype=jnp.int32)[None, :] == accepted[:, None]).astype(
        jnp.float32
    )
    reached = jnp.einsum("ra,rah->rh", count_pick, before, precision=highest)
    valid = positions[None, :] < accepted[:, None]
    exponent = jnp.where(valid[:, :, None], reached[:, None, :] - inclusive, -jnp.inf)
    token_weight = jnp.exp(exponent) * step_size
    weighted_x = token_weight[:, :, :, None] * x_heads
    retained = jnp.exp(reached)[:, :, None, None] * initial + jnp.einsum(
        "rshp,rshn->rhpn", weighted_x, b_heads, precision=highest
    )
    retained = retained.astype(jnp.bfloat16)
    gated = y_values.reshape(local_requests, L, local_heads * P_SIZE) * jax.nn.silu(
        z_input.astype(jnp.float32)
    )
    blocks = gated.reshape(local_requests, L, local_heads, P_SIZE)
    inverse_rms = lax.rsqrt(jnp.mean(blocks * blocks, axis=3, keepdims=True) + epsilon)
    normed = (
        (blocks * inverse_rms).reshape(local_requests, L, local_heads * P_SIZE)
        * norm_gain[None, None, :]
    ).astype(jnp.bfloat16)
    partial_terms = jnp.dot(
        normed.reshape(local_requests * L, local_heads * P_SIZE),
        out_weight,
        preferred_element_type=jnp.float32,
    )
    share_width = D // lax.axis_size("head")
    share = lax.psum_scatter(partial_terms, "head", scatter_dimension=1, tiled=True)
    mixed = share.astype(jnp.bfloat16).reshape(local_requests, L, share_width)
    window_rows = jnp.arange(K - 1 + L, dtype=jnp.int32)
    row_pick = (
        window_rows[None, None, :]
        == accepted[:, None, None] + jnp.arange(K - 1, dtype=jnp.int32)[None, :, None]
    ).astype(jnp.bfloat16)
    kept_x = jnp.einsum(
        "rkt,rtc->rkc", row_pick, x_joined, preferred_element_type=jnp.float32
    ).astype(jnp.bfloat16)
    kept_bc = jnp.einsum(
        "rkt,rtc->rkc", row_pick, bc_joined, preferred_element_type=jnp.float32
    ).astype(jnp.bfloat16)
    requests_per_owner = local_requests
    owners = lax.axis_size("req")
    cap = min(CAP, local_requests)
    request_ids = jnp.arange(all_requests, dtype=jnp.int32)
    source = request_ids // requests_per_owner
    same_owner = next_owner[:, None] == next_owner[None, :]
    earlier = request_ids[None, :] < request_ids[:, None]
    rank_at_owner = jnp.sum((same_owner & earlier).astype(jnp.int32), axis=1)
    same_source = source[:, None] == source[None, :]
    rank_in_pair = jnp.sum((same_owner & earlier & same_source).astype(jnp.int32), axis=1)
    local_owner = lax.dynamic_slice_in_dim(next_owner, req_index * local_requests, local_requests)
    local_rank = lax.dynamic_slice_in_dim(rank_in_pair, req_index * local_requests, local_requests)
    slot_rows = jnp.arange(local_requests, dtype=jnp.int32)
    chosen = (local_owner[None, None, :] == jnp.arange(owners, dtype=jnp.int32)[:, None, None]) & (
        local_rank[None, None, :] == jnp.arange(cap, dtype=jnp.int32)[None, :, None]
    )
    send_index = jnp.sum(jnp.where(chosen, slot_rows[None, None, :], 0), axis=2).reshape(-1)
    arriving = (next_owner[None, :] == req_index) & (rank_at_owner[None, :] == slot_rows[:, None])
    receive_index = jnp.sum(
        jnp.where(arriving, source[None, :] * cap + rank_in_pair[None, :], 0), axis=1
    )

    partner_bits = range(1, owners)
    own_index = jnp.take(send_index.reshape(owners, cap), req_index, axis=0)
    pair_index = [
        jnp.take(send_index.reshape(owners, cap), req_index ^ bits, axis=0) for bits in partner_bits
    ]
    arriving_source = jnp.sum(jnp.where(arriving, source[None, :], 0), axis=1)
    arriving_rank = jnp.sum(jnp.where(arriving, rank_in_pair[None, :], 0), axis=1)
    gather_index = (arriving_source ^ req_index) * cap + arriving_rank

    def send_pieces(values):
        pieces = [jnp.take(values, own_index, axis=0, mode="clip")]
        for bits, index in zip(partner_bits, pair_index):
            outgoing = jnp.take(values, index, axis=0, mode="clip")
            pairs = [(i, i ^ bits) for i in range(owners)]
            pieces.append(lax.ppermute(outgoing, "req", pairs))
        return pieces

    def hand_over(values):
        pieces = send_pieces(values)
        return jnp.take(jnp.concatenate(pieces, axis=0), gather_index, axis=0, mode="clip")

    owner_ids = jnp.arange(owners, dtype=jnp.int32)
    pair_count = jnp.sum(
        (
            (source[None, None, :] == owner_ids[:, None, None])
            & (next_owner[None, None, :] == owner_ids[None, :, None])
        ).astype(jnp.int32),
        axis=2,
    )
    first_slots = min(3, cap)
    state_pieces = [jnp.take(retained, own_index, axis=0, mode="clip")]
    for bits, index in zip(partner_bits, pair_index):
        pairs = [(i, i ^ bits) for i in range(owners)]
        if bits == 1:
            outgoing = jnp.take(retained, index, axis=0, mode="clip")
            state_pieces.append(lax.ppermute(outgoing, "req", pairs))
            continue
        outgoing = jnp.take(retained, index[:first_slots], axis=0, mode="clip")
        arrived = lax.ppermute(outgoing, "req", pairs)
        buffer = jnp.concatenate(
            [arrived, jnp.zeros((cap - first_slots,) + arrived.shape[1:], arrived.dtype)], axis=0
        )
        needed = jnp.max(pair_count[owner_ids, owner_ids ^ bits])
        needed = jnp.clip(lax.pmax(needed, "group"), first_slots, cap)

        def one_slot(slot, held, index=index, pairs=pairs):
            row = lax.dynamic_index_in_dim(retained, index[slot], 0, keepdims=True)
            got = lax.ppermute(row, "req", pairs)
            return lax.dynamic_update_index_in_dim(held, got, slot, 0)

        state_pieces.append(lax.fori_loop(first_slots, needed, one_slot, buffer))
    new_ssm_state = jnp.take(
        jnp.concatenate(state_pieces, axis=0), gather_index, axis=0, mode="clip"
    )
    new_conv_x_state = hand_over(kept_x)
    new_conv_bc_state = hand_over(kept_bc)
    return (mixed, new_ssm_state, new_conv_x_state, new_conv_bc_state)


def solution(mesh):
    placed = (
        P(("group", "req"), None, "head"),
        P(("group", "req"), None, "head"),
        P(("group", "req"), None, None),
        P(("group", "req"), None, "head"),
        P(("group", "req"), None, "head"),
        P(("group", "req"), None, None),
        P(("group", "req"), "head", None, None),
        P(("group", "req")),
        P("group"),
        P(None, "head"),
        P("head"),
        P(),
        P(),
        P("head"),
        P("head"),
        P("head"),
        P("head"),
        P("head", None),
    )
    return jax.shard_map(
        on_device,
        mesh=mesh,
        in_specs=placed,
        out_specs=(
            P(("group", "req"), None, "head"),
            P(("group", "req"), "head", None, None),
            P(("group", "req"), None, "head"),
            P(("group", "req"), None, None),
        ),
        check_vma=False,
    )
```

```python
import jax
import jax.numpy as jnp
from jax import lax
from jax.sharding import PartitionSpec as P

D = 8192
H = 256
P_SIZE = 64
N = 256
G = 8
K = 4
L = 8
CAP = 8


epsilon = 1e-05
highest = lax.Precision.HIGH


def conv_window(history, inputs, weight, bias_vector):
    joined = jnp.concatenate([history, inputs], axis=1)
    widened = joined.astype(jnp.float32)
    accumulated = bias_vector[None, None, :] + weight[0][None, None, :] * widened[:, 0:L, :]
    for offset in range(1, K):
        accumulated = (
            accumulated + weight[offset][None, None, :] * widened[:, offset : offset + L, :]
        )
    return (jax.nn.silu(accumulated), joined)


def on_device(
    x_input,
    z_input,
    bc_input,
    dt_input,
    conv_x_state,
    conv_bc_state,
    ssm_state,
    accepted,
    next_owner,
    conv_x_weight,
    conv_x_bias,
    conv_bc_weight,
    conv_bc_bias,
    dt_bias,
    a_log,
    d_skip,
    norm_gain,
    out_weight,
):
    local_requests = x_input.shape[0]
    local_heads = dt_input.shape[2]
    head_index = lax.axis_index("head")
    req_index = lax.axis_index("req")
    all_requests = next_owner.shape[0]
    heads_group = H // G
    x_conv, x_joined = conv_window(conv_x_state, x_input, conv_x_weight, conv_x_bias)
    bc_conv, bc_joined = conv_window(conv_bc_state, bc_input, conv_bc_weight, conv_bc_bias)
    step_size = jax.nn.softplus(dt_input + dt_bias[None, None, :])
    log_decay = -jnp.exp(a_log)[None, None, :] * step_size
    global_heads = head_index * local_heads + jnp.arange(local_heads, dtype=jnp.int32)
    group_pick = (
        global_heads[:, None] // heads_group == jnp.arange(G, dtype=jnp.int32)[None, :]
    ).astype(jnp.float32)
    b_groups = bc_conv[:, :, : G * N].reshape(local_requests, L, G, N)
    c_groups = bc_conv[:, :, G * N :].reshape(local_requests, L, G, N)
    b_heads = jnp.einsum("rlgn,hg->rlhn", b_groups, group_pick, precision=highest)
    c_heads = jnp.einsum("rlgn,hg->rlhn", c_groups, group_pick, precision=highest)
    x_heads = x_conv.reshape(local_requests, L, local_heads, P_SIZE)
    initial = ssm_state.astype(jnp.float32)
    inclusive = jnp.cumsum(log_decay, axis=1)
    before = jnp.concatenate(
        [jnp.zeros((local_requests, 1, local_heads), jnp.float32), inclusive], axis=1
    )
    positions = jnp.arange(L, dtype=jnp.int32)
    causal = positions[:, None] >= positions[None, :]
    by_head = inclusive.transpose(0, 2, 1)
    differences = by_head[:, :, :, None] - by_head[:, :, None, :]
    pair_decay = jnp.exp(jnp.where(causal[None, None], differences, -jnp.inf))
    count_pick = (jnp.arange(L + 1, dtype=jnp.int32)[None, :] == accepted[:, None]).astype(
        jnp.float32
    )
    reached = jnp.einsum("ra,rah->rh", count_pick, before, precision=highest)
    valid = positions[None, :] < accepted[:, None]
    exponent = jnp.where(valid[:, :, None], reached[:, None, :] - inclusive, -jnp.inf)
    token_weight = jnp.exp(exponent) * step_size
    weighted_x = token_weight[:, :, :, None] * x_heads
    retained = jnp.exp(reached)[:, :, None, None] * initial + jnp.einsum(
        "rshp,rshn->rhpn", weighted_x, b_heads, precision=highest
    )
    retained = retained.astype(jnp.bfloat16)
    window_rows = jnp.arange(K - 1 + L, dtype=jnp.int32)
    row_pick = (
        window_rows[None, None, :]
        == accepted[:, None, None] + jnp.arange(K - 1, dtype=jnp.int32)[None, :, None]
    ).astype(jnp.bfloat16)
    kept_x = jnp.einsum(
        "rkt,rtc->rkc", row_pick, x_joined, preferred_element_type=jnp.float32
    ).astype(jnp.bfloat16)
    kept_bc = jnp.einsum(
        "rkt,rtc->rkc", row_pick, bc_joined, preferred_element_type=jnp.float32
    ).astype(jnp.bfloat16)
    requests_per_owner = local_requests
    owners = lax.axis_size("req")
    cap = min(CAP, local_requests)
    request_ids = jnp.arange(all_requests, dtype=jnp.int32)
    source = request_ids // requests_per_owner
    same_owner = next_owner[:, None] == next_owner[None, :]
    earlier = request_ids[None, :] < request_ids[:, None]
    rank_at_owner = jnp.sum((same_owner & earlier).astype(jnp.int32), axis=1)
    same_source = source[:, None] == source[None, :]
    rank_in_pair = jnp.sum((same_owner & earlier & same_source).astype(jnp.int32), axis=1)
    local_owner = lax.dynamic_slice_in_dim(next_owner, req_index * local_requests, local_requests)
    local_rank = lax.dynamic_slice_in_dim(rank_in_pair, req_index * local_requests, local_requests)
    slot_rows = jnp.arange(local_requests, dtype=jnp.int32)
    chosen = (local_owner[None, None, :] == jnp.arange(owners, dtype=jnp.int32)[:, None, None]) & (
        local_rank[None, None, :] == jnp.arange(cap, dtype=jnp.int32)[None, :, None]
    )
    send_index = jnp.sum(jnp.where(chosen, slot_rows[None, None, :], 0), axis=2).reshape(-1)
    arriving = (next_owner[None, :] == req_index) & (rank_at_owner[None, :] == slot_rows[:, None])
    receive_index = jnp.sum(
        jnp.where(arriving, source[None, :] * cap + rank_in_pair[None, :], 0), axis=1
    )

    partner_bits = range(1, owners)
    own_index = jnp.take(send_index.reshape(owners, cap), req_index, axis=0)
    pair_index = [
        jnp.take(send_index.reshape(owners, cap), req_index ^ bits, axis=0) for bits in partner_bits
    ]
    arriving_source = jnp.sum(jnp.where(arriving, source[None, :], 0), axis=1)
    arriving_rank = jnp.sum(jnp.where(arriving, rank_in_pair[None, :], 0), axis=1)
    gather_index = (arriving_source ^ req_index) * cap + arriving_rank

    piece_of = jnp.clip(arriving_source ^ req_index, 0, owners - 1)
    slot_of = jnp.clip(arriving_rank, 0, cap - 1)

    def send_pieces(values):
        pieces = [jnp.take(values, own_index, axis=0, mode="clip")]
        for bits, index in zip(partner_bits, pair_index):
            outgoing = jnp.take(values, index, axis=0, mode="clip")
            pairs = [(i, i ^ bits) for i in range(owners)]
            pieces.append(lax.ppermute(outgoing, "req", pairs))
        return pieces

    def assemble_rows(pieces):
        def pick(which):
            return lambda slot: lax.dynamic_index_in_dim(pieces[which], slot, 0, keepdims=True)

        def place(row, held):
            chosen = lax.switch(piece_of[row], [pick(w) for w in range(len(pieces))], slot_of[row])
            return lax.dynamic_update_index_in_dim(held, chosen, row, 0)

        empty = jnp.zeros((local_requests,) + pieces[0].shape[1:], pieces[0].dtype)
        return lax.fori_loop(0, local_requests, place, empty)

    def hand_over(values):
        pieces = send_pieces(values)
        return jnp.take(jnp.concatenate(pieces, axis=0), gather_index, axis=0, mode="clip")

    owner_ids = jnp.arange(owners, dtype=jnp.int32)
    pair_count = jnp.sum(
        (
            (source[None, None, :] == owner_ids[:, None, None])
            & (next_owner[None, None, :] == owner_ids[None, :, None])
        ).astype(jnp.int32),
        axis=2,
    )
    first_slots = min(3, cap)
    cross_pieces = []
    state_pieces = [jnp.take(retained, own_index, axis=0, mode="clip")]
    for bits, index in zip(partner_bits, pair_index):
        pairs = [(i, i ^ bits) for i in range(owners)]
        if bits == 1:
            near_pairs, near_index = pairs, index
            state_pieces.append(None)
            continue
        outgoing = jnp.take(retained, index[:first_slots], axis=0, mode="clip")
        cross_pieces.append(outgoing)
        arrived = lax.ppermute(outgoing, "req", pairs)
        buffer = jnp.concatenate(
            [arrived, jnp.zeros((cap - first_slots,) + arrived.shape[1:], arrived.dtype)], axis=0
        )
        needed = jnp.max(pair_count[owner_ids, owner_ids ^ bits])
        needed = jnp.clip(lax.pmax(needed, "group"), first_slots, cap)

        def one_slot(slot, held, index=index, pairs=pairs):
            row = lax.dynamic_index_in_dim(retained, index[slot], 0, keepdims=True)
            got = lax.ppermute(row, "req", pairs)
            return lax.dynamic_update_index_in_dim(held, got, slot, 0)

        state_pieces.append(lax.fori_loop(first_slots, needed, one_slot, buffer))
    x_heads, c_heads, b_heads, cross_pieces, near_source = lax.optimization_barrier(
        (x_heads, c_heads, b_heads, cross_pieces, retained)
    )
    near_outgoing = jnp.take(near_source, near_index, axis=0, mode="clip")
    state_pieces[1] = lax.ppermute(near_outgoing, "req", near_pairs)
    scores = jnp.einsum("rthn,rshn->rhts", c_heads, b_heads, precision=highest)
    weights = scores * pair_decay * step_size.transpose(0, 2, 1)[:, :, None, :]
    within = jnp.einsum("rhts,rshp->rthp", weights, x_heads, precision=highest)
    carried = jnp.exp(inclusive)[:, :, :, None] * jnp.einsum(
        "rhpn,rthn->rthp", initial, c_heads, precision=highest
    )
    y_values = within + carried + d_skip[None, None, :, None] * x_heads
    gated = y_values.reshape(local_requests, L, local_heads * P_SIZE) * jax.nn.silu(
        z_input.astype(jnp.float32)
    )
    blocks = gated.reshape(local_requests, L, local_heads, P_SIZE)
    inverse_rms = lax.rsqrt(jnp.mean(blocks * blocks, axis=3, keepdims=True) + epsilon)
    normed = (
        (blocks * inverse_rms).reshape(local_requests, L, local_heads * P_SIZE)
        * norm_gain[None, None, :]
    ).astype(jnp.bfloat16)
    partial_terms = jnp.dot(
        normed.reshape(local_requests * L, local_heads * P_SIZE),
        out_weight,
        preferred_element_type=jnp.float32,
    )
    share_width = D // lax.axis_size("head")
    share = lax.psum_scatter(partial_terms, "head", scatter_dimension=1, tiled=True)
    mixed = share.astype(jnp.bfloat16).reshape(local_requests, L, share_width)
    new_ssm_state = assemble_rows(state_pieces)
    new_conv_x_state = hand_over(kept_x)
    new_conv_bc_state = hand_over(kept_bc)
    return (mixed, new_ssm_state, new_conv_x_state, new_conv_bc_state)


def solution(mesh):
    placed = (
        P(("group", "req"), None, "head"),
        P(("group", "req"), None, "head"),
        P(("group", "req"), None, None),
        P(("group", "req"), None, "head"),
        P(("group", "req"), None, "head"),
        P(("group", "req"), None, None),
        P(("group", "req"), "head", None, None),
        P(("group", "req")),
        P("group"),
        P(None, "head"),
        P("head"),
        P(),
        P(),
        P("head"),
        P("head"),
        P("head"),
        P("head"),
        P("head", None),
    )
    return jax.shard_map(
        on_device,
        mesh=mesh,
        in_specs=placed,
        out_specs=(
            P(("group", "req"), None, "head"),
            P(("group", "req"), "head", None, None),
            P(("group", "req"), None, "head"),
            P(("group", "req"), None, None),
        ),
        check_vma=False,
    )
```

```python
import jax
import jax.numpy as jnp
from jax import lax
from jax.sharding import PartitionSpec as P

D = 8192
H = 256
P_SIZE = 64
N = 256
G = 8
K = 4
L = 8
CAP = 8


epsilon = 1e-05
highest = lax.Precision.HIGH


def conv_window(history, inputs, weight, bias_vector):
    joined = jnp.concatenate([history, inputs], axis=1)
    widened = joined.astype(jnp.float32)
    accumulated = bias_vector[None, None, :] + weight[0][None, None, :] * widened[:, 0:L, :]
    for offset in range(1, K):
        accumulated = (
            accumulated + weight[offset][None, None, :] * widened[:, offset : offset + L, :]
        )
    return (jax.nn.silu(accumulated), joined)


def on_device(
    x_input,
    z_input,
    bc_input,
    dt_input,
    conv_x_state,
    conv_bc_state,
    ssm_state,
    accepted,
    next_owner,
    conv_x_weight,
    conv_x_bias,
    conv_bc_weight,
    conv_bc_bias,
    dt_bias,
    a_log,
    d_skip,
    norm_gain,
    out_weight,
):
    local_requests = x_input.shape[0]
    local_heads = dt_input.shape[2]
    head_index = lax.axis_index("head")
    req_index = lax.axis_index("req")
    all_requests = next_owner.shape[0]
    heads_group = H // G
    x_conv, x_joined = conv_window(conv_x_state, x_input, conv_x_weight, conv_x_bias)
    bc_conv, bc_joined = conv_window(conv_bc_state, bc_input, conv_bc_weight, conv_bc_bias)
    step_size = jax.nn.softplus(dt_input + dt_bias[None, None, :])
    log_decay = -jnp.exp(a_log)[None, None, :] * step_size
    global_heads = head_index * local_heads + jnp.arange(local_heads, dtype=jnp.int32)
    group_pick = (
        global_heads[:, None] // heads_group == jnp.arange(G, dtype=jnp.int32)[None, :]
    ).astype(jnp.float32)
    b_groups = bc_conv[:, :, : G * N].reshape(local_requests, L, G, N)
    c_groups = bc_conv[:, :, G * N :].reshape(local_requests, L, G, N)
    b_heads = jnp.einsum("rlgn,hg->rlhn", b_groups, group_pick, precision=highest)
    c_heads = jnp.einsum("rlgn,hg->rlhn", c_groups, group_pick, precision=highest)
    x_heads = x_conv.reshape(local_requests, L, local_heads, P_SIZE)
    initial = ssm_state.astype(jnp.float32)
    inclusive = jnp.cumsum(log_decay, axis=1)
    before = jnp.concatenate(
        [jnp.zeros((local_requests, 1, local_heads), jnp.float32), inclusive], axis=1
    )
    positions = jnp.arange(L, dtype=jnp.int32)
    causal = positions[:, None] >= positions[None, :]
    by_head = inclusive.transpose(0, 2, 1)
    differences = by_head[:, :, :, None] - by_head[:, :, None, :]
    pair_decay = jnp.exp(jnp.where(causal[None, None], differences, -jnp.inf))
    scores = jnp.einsum("rthn,rshn->rhts", c_heads, b_heads, precision=highest)
    weights = scores * pair_decay * step_size.transpose(0, 2, 1)[:, :, None, :]
    within = jnp.einsum("rhts,rshp->rthp", weights, x_heads, precision=highest)
    carried = jnp.exp(inclusive)[:, :, :, None] * jnp.einsum(
        "rhpn,rthn->rthp", initial, c_heads, precision=highest
    )
    y_values = within + carried + d_skip[None, None, :, None] * x_heads
    count_pick = (jnp.arange(L + 1, dtype=jnp.int32)[None, :] == accepted[:, None]).astype(
        jnp.float32
    )
    reached = jnp.einsum("ra,rah->rh", count_pick, before, precision=highest)
    valid = positions[None, :] < accepted[:, None]
    exponent = jnp.where(valid[:, :, None], reached[:, None, :] - inclusive, -jnp.inf)
    token_weight = jnp.exp(exponent) * step_size
    weighted_x = token_weight[:, :, :, None] * x_heads
    retained = jnp.exp(reached)[:, :, None, None] * initial + jnp.einsum(
        "rshp,rshn->rhpn", weighted_x, b_heads, precision=highest
    )
    retained = retained.astype(jnp.bfloat16)
    gated = y_values.reshape(local_requests, L, local_heads * P_SIZE) * jax.nn.silu(
        z_input.astype(jnp.float32)
    )
    blocks = gated.reshape(local_requests, L, local_heads, P_SIZE)
    inverse_rms = lax.rsqrt(jnp.mean(blocks * blocks, axis=3, keepdims=True) + epsilon)
    normed = (
        (blocks * inverse_rms).reshape(local_requests, L, local_heads * P_SIZE)
        * norm_gain[None, None, :]
    ).astype(jnp.bfloat16)
    partial_terms = jnp.dot(
        normed.reshape(local_requests * L, local_heads * P_SIZE),
        out_weight,
        preferred_element_type=jnp.float32,
    )
    share_width = D // lax.axis_size("head")
    share = lax.psum_scatter(partial_terms, "head", scatter_dimension=1, tiled=True)
    mixed = share.astype(jnp.bfloat16).reshape(local_requests, L, share_width)
    window_rows = jnp.arange(K - 1 + L, dtype=jnp.int32)
    row_pick = (
        window_rows[None, None, :]
        == accepted[:, None, None] + jnp.arange(K - 1, dtype=jnp.int32)[None, :, None]
    ).astype(jnp.bfloat16)
    kept_x = jnp.einsum(
        "rkt,rtc->rkc", row_pick, x_joined, preferred_element_type=jnp.float32
    ).astype(jnp.bfloat16)
    kept_bc = jnp.einsum(
        "rkt,rtc->rkc", row_pick, bc_joined, preferred_element_type=jnp.float32
    ).astype(jnp.bfloat16)
    requests_per_owner = local_requests
    owners = lax.axis_size("req")
    cap = min(CAP, local_requests)
    request_ids = jnp.arange(all_requests, dtype=jnp.int32)
    source = request_ids // requests_per_owner
    same_owner = next_owner[:, None] == next_owner[None, :]
    earlier = request_ids[None, :] < request_ids[:, None]
    rank_at_owner = jnp.sum((same_owner & earlier).astype(jnp.int32), axis=1)
    same_source = source[:, None] == source[None, :]
    rank_in_pair = jnp.sum((same_owner & earlier & same_source).astype(jnp.int32), axis=1)
    local_owner = lax.dynamic_slice_in_dim(next_owner, req_index * local_requests, local_requests)
    local_rank = lax.dynamic_slice_in_dim(rank_in_pair, req_index * local_requests, local_requests)
    slot_rows = jnp.arange(local_requests, dtype=jnp.int32)
    chosen = (local_owner[None, None, :] == jnp.arange(owners, dtype=jnp.int32)[:, None, None]) & (
        local_rank[None, None, :] == jnp.arange(cap, dtype=jnp.int32)[None, :, None]
    )
    send_index = jnp.sum(jnp.where(chosen, slot_rows[None, None, :], 0), axis=2).reshape(-1)
    arriving = (next_owner[None, :] == req_index) & (rank_at_owner[None, :] == slot_rows[:, None])
    receive_index = jnp.sum(
        jnp.where(arriving, source[None, :] * cap + rank_in_pair[None, :], 0), axis=1
    )

    partner_bits = range(1, owners)
    own_index = jnp.take(send_index.reshape(owners, cap), req_index, axis=0)
    pair_index = [
        jnp.take(send_index.reshape(owners, cap), req_index ^ bits, axis=0) for bits in partner_bits
    ]
    arriving_source = jnp.sum(jnp.where(arriving, source[None, :], 0), axis=1)
    arriving_rank = jnp.sum(jnp.where(arriving, rank_in_pair[None, :], 0), axis=1)
    gather_index = (arriving_source ^ req_index) * cap + arriving_rank

    def send_pieces(values):
        pieces = [jnp.take(values, own_index, axis=0, mode="clip")]
        for bits, index in zip(partner_bits, pair_index):
            outgoing = jnp.take(values, index, axis=0, mode="clip")
            pairs = [(i, i ^ bits) for i in range(owners)]
            pieces.append(lax.ppermute(outgoing, "req", pairs))
        return pieces

    def hand_over(values):
        pieces = send_pieces(values)
        return jnp.take(jnp.concatenate(pieces, axis=0), gather_index, axis=0, mode="clip")

    owner_ids = jnp.arange(owners, dtype=jnp.int32)
    pair_count = jnp.sum(
        (
            (source[None, None, :] == owner_ids[:, None, None])
            & (next_owner[None, None, :] == owner_ids[None, :, None])
        ).astype(jnp.int32),
        axis=2,
    )
    first_slots = min(3, cap)
    state_pieces = [jnp.take(retained, own_index, axis=0, mode="clip")]
    first_index = send_index.reshape(owners, cap)[:, :first_slots].reshape(-1)
    first_arrivals = lax.all_to_all(
        jnp.take(retained, first_index, axis=0, mode="clip"), "req", 0, 0, tiled=True
    )
    for bits, index in zip(partner_bits, pair_index):
        pairs = [(i, i ^ bits) for i in range(owners)]
        if bits == 1:
            outgoing = jnp.take(retained, index, axis=0, mode="clip")
            state_pieces.append(lax.ppermute(outgoing, "req", pairs))
            continue
        arrived = lax.dynamic_slice_in_dim(
            first_arrivals, (req_index ^ bits) * first_slots, first_slots, 0
        )
        buffer = jnp.concatenate(
            [arrived, jnp.zeros((cap - first_slots,) + arrived.shape[1:], arrived.dtype)], axis=0
        )
        needed = jnp.max(pair_count[owner_ids, owner_ids ^ bits])
        needed = jnp.clip(lax.pmax(needed, "group"), first_slots, cap)

        def one_slot(slot, held, index=index, pairs=pairs):
            row = lax.dynamic_index_in_dim(retained, index[slot], 0, keepdims=True)
            got = lax.ppermute(row, "req", pairs)
            return lax.dynamic_update_index_in_dim(held, got, slot, 0)

        state_pieces.append(lax.fori_loop(first_slots, needed, one_slot, buffer))
    new_ssm_state = jnp.take(
        jnp.concatenate(state_pieces, axis=0), gather_index, axis=0, mode="clip"
    )
    new_conv_x_state = hand_over(kept_x)
    new_conv_bc_state = hand_over(kept_bc)
    return (mixed, new_ssm_state, new_conv_x_state, new_conv_bc_state)


def solution(mesh):
    placed = (
        P(("group", "req"), None, "head"),
        P(("group", "req"), None, "head"),
        P(("group", "req"), None, None),
        P(("group", "req"), None, "head"),
        P(("group", "req"), None, "head"),
        P(("group", "req"), None, None),
        P(("group", "req"), "head", None, None),
        P(("group", "req")),
        P("group"),
        P(None, "head"),
        P("head"),
        P(),
        P(),
        P("head"),
        P("head"),
        P("head"),
        P("head"),
        P("head", None),
    )
    return jax.shard_map(
        on_device,
        mesh=mesh,
        in_specs=placed,
        out_specs=(
            P(("group", "req"), None, "head"),
            P(("group", "req"), "head", None, None),
            P(("group", "req"), None, "head"),
            P(("group", "req"), None, None),
        ),
        check_vma=False,
    )
```

```python
import jax
import jax.numpy as jnp
from jax import lax
from jax.sharding import PartitionSpec as P

D = 8192
H = 256
P_SIZE = 64
N = 256
G = 8
K = 4
L = 8
CAP = 8


epsilon = 1e-05
highest = lax.Precision.HIGH


def conv_window(history, inputs, weight, bias_vector):
    joined = jnp.concatenate([history, inputs], axis=1)
    widened = joined.astype(jnp.float32)
    accumulated = bias_vector[None, None, :] + weight[0][None, None, :] * widened[:, 0:L, :]
    for offset in range(1, K):
        accumulated = (
            accumulated + weight[offset][None, None, :] * widened[:, offset : offset + L, :]
        )
    return (jax.nn.silu(accumulated), joined)


def on_device(
    x_input,
    z_input,
    bc_input,
    dt_input,
    conv_x_state,
    conv_bc_state,
    ssm_state,
    accepted,
    next_owner,
    conv_x_weight,
    conv_x_bias,
    conv_bc_weight,
    conv_bc_bias,
    dt_bias,
    a_log,
    d_skip,
    norm_gain,
    out_weight,
):
    local_requests = x_input.shape[0]
    local_heads = dt_input.shape[2]
    head_index = lax.axis_index("head")
    req_index = lax.axis_index("req")
    all_requests = next_owner.shape[0]
    heads_group = H // G
    x_conv, x_joined = conv_window(conv_x_state, x_input, conv_x_weight, conv_x_bias)
    bc_conv, bc_joined = conv_window(conv_bc_state, bc_input, conv_bc_weight, conv_bc_bias)
    step_size = jax.nn.softplus(dt_input + dt_bias[None, None, :])
    log_decay = -jnp.exp(a_log)[None, None, :] * step_size
    global_heads = head_index * local_heads + jnp.arange(local_heads, dtype=jnp.int32)
    group_pick = (
        global_heads[:, None] // heads_group == jnp.arange(G, dtype=jnp.int32)[None, :]
    ).astype(jnp.float32)
    b_groups = bc_conv[:, :, : G * N].reshape(local_requests, L, G, N)
    c_groups = bc_conv[:, :, G * N :].reshape(local_requests, L, G, N)
    b_heads = jnp.einsum("rlgn,hg->rlhn", b_groups, group_pick, precision=highest)
    c_heads = jnp.einsum("rlgn,hg->rlhn", c_groups, group_pick, precision=highest)
    x_heads = x_conv.reshape(local_requests, L, local_heads, P_SIZE)
    initial = ssm_state.astype(jnp.float32)
    inclusive = jnp.cumsum(log_decay, axis=1)
    before = jnp.concatenate(
        [jnp.zeros((local_requests, 1, local_heads), jnp.float32), inclusive], axis=1
    )
    positions = jnp.arange(L, dtype=jnp.int32)
    causal = positions[:, None] >= positions[None, :]
    by_head = inclusive.transpose(0, 2, 1)
    differences = by_head[:, :, :, None] - by_head[:, :, None, :]
    pair_decay = jnp.exp(jnp.where(causal[None, None], differences, -jnp.inf))
    scores = jnp.einsum("rthn,rshn->rhts", c_heads, b_heads, precision=highest)
    weights = scores * pair_decay * step_size.transpose(0, 2, 1)[:, :, None, :]
    within = jnp.einsum("rhts,rshp->rthp", weights, x_heads, precision=highest)
    carried = jnp.exp(inclusive)[:, :, :, None] * jnp.einsum(
        "rhpn,rthn->rthp", initial, c_heads, precision=highest
    )
    y_values = within + carried + d_skip[None, None, :, None] * x_heads
    count_pick = (jnp.arange(L + 1, dtype=jnp.int32)[None, :] == accepted[:, None]).astype(
        jnp.float32
    )
    reached = jnp.einsum("ra,rah->rh", count_pick, before, precision=highest)
    valid = positions[None, :] < accepted[:, None]
    exponent = jnp.where(valid[:, :, None], reached[:, None, :] - inclusive, -jnp.inf)
    token_weight = jnp.exp(exponent) * step_size
    weighted_x = token_weight[:, :, :, None] * x_heads
    retained = jnp.exp(reached)[:, :, None, None] * initial + jnp.einsum(
        "rshp,rshn->rhpn", weighted_x, b_heads, precision=highest
    )
    retained = retained.astype(jnp.bfloat16)
    gated = y_values.reshape(local_requests, L, local_heads * P_SIZE) * jax.nn.silu(
        z_input.astype(jnp.float32)
    )
    blocks = gated.reshape(local_requests, L, local_heads, P_SIZE)
    inverse_rms = lax.rsqrt(jnp.mean(blocks * blocks, axis=3, keepdims=True) + epsilon)
    normed = (
        (blocks * inverse_rms).reshape(local_requests, L, local_heads * P_SIZE)
        * norm_gain[None, None, :]
    ).astype(jnp.bfloat16)
    partial_terms = jnp.dot(
        normed.reshape(local_requests * L, local_heads * P_SIZE),
        out_weight,
        preferred_element_type=jnp.float32,
    )
    share_width = D // lax.axis_size("head")
    share = lax.psum_scatter(partial_terms, "head", scatter_dimension=1, tiled=True)
    mixed = share.astype(jnp.bfloat16).reshape(local_requests, L, share_width)
    window_rows = jnp.arange(K - 1 + L, dtype=jnp.int32)
    row_pick = (
        window_rows[None, None, :]
        == accepted[:, None, None] + jnp.arange(K - 1, dtype=jnp.int32)[None, :, None]
    ).astype(jnp.bfloat16)
    kept_x = jnp.einsum(
        "rkt,rtc->rkc", row_pick, x_joined, preferred_element_type=jnp.float32
    ).astype(jnp.bfloat16)
    kept_bc = jnp.einsum(
        "rkt,rtc->rkc", row_pick, bc_joined, preferred_element_type=jnp.float32
    ).astype(jnp.bfloat16)
    requests_per_owner = local_requests
    owners = lax.axis_size("req")
    cap = min(CAP, local_requests)
    request_ids = jnp.arange(all_requests, dtype=jnp.int32)
    source = request_ids // requests_per_owner
    same_owner = next_owner[:, None] == next_owner[None, :]
    earlier = request_ids[None, :] < request_ids[:, None]
    rank_at_owner = jnp.sum((same_owner & earlier).astype(jnp.int32), axis=1)
    same_source = source[:, None] == source[None, :]
    rank_in_pair = jnp.sum((same_owner & earlier & same_source).astype(jnp.int32), axis=1)
    local_owner = lax.dynamic_slice_in_dim(next_owner, req_index * local_requests, local_requests)
    local_rank = lax.dynamic_slice_in_dim(rank_in_pair, req_index * local_requests, local_requests)
    slot_rows = jnp.arange(local_requests, dtype=jnp.int32)
    chosen = (local_owner[None, None, :] == jnp.arange(owners, dtype=jnp.int32)[:, None, None]) & (
        local_rank[None, None, :] == jnp.arange(cap, dtype=jnp.int32)[None, :, None]
    )
    send_index = jnp.sum(jnp.where(chosen, slot_rows[None, None, :], 0), axis=2).reshape(-1)
    arriving = (next_owner[None, :] == req_index) & (rank_at_owner[None, :] == slot_rows[:, None])
    receive_index = jnp.sum(
        jnp.where(arriving, source[None, :] * cap + rank_in_pair[None, :], 0), axis=1
    )

    partner_bits = range(1, owners)
    own_index = jnp.take(send_index.reshape(owners, cap), req_index, axis=0)
    pair_index = [
        jnp.take(send_index.reshape(owners, cap), req_index ^ bits, axis=0) for bits in partner_bits
    ]
    arriving_source = jnp.sum(jnp.where(arriving, source[None, :], 0), axis=1)
    arriving_rank = jnp.sum(jnp.where(arriving, rank_in_pair[None, :], 0), axis=1)
    gather_index = (arriving_source ^ req_index) * cap + arriving_rank

    def send_pieces(values):
        pieces = [jnp.take(values, own_index, axis=0, mode="clip")]
        for bits, index in zip(partner_bits, pair_index):
            outgoing = jnp.take(values, index, axis=0, mode="clip")
            pairs = [(i, i ^ bits) for i in range(owners)]
            pieces.append(lax.ppermute(outgoing, "req", pairs))
        return pieces

    def hand_over(values):
        pieces = send_pieces(values)
        return jnp.take(jnp.concatenate(pieces, axis=0), gather_index, axis=0, mode="clip")

    owner_ids = jnp.arange(owners, dtype=jnp.int32)
    pair_count = jnp.sum(
        (
            (source[None, None, :] == owner_ids[:, None, None])
            & (next_owner[None, None, :] == owner_ids[None, :, None])
        ).astype(jnp.int32),
        axis=2,
    )
    first_slots = min(3, cap)
    state_pieces = [jnp.take(retained, own_index, axis=0, mode="clip")]
    first_index = send_index.reshape(owners, cap)[:, :first_slots].reshape(-1)
    first_arrivals = lax.all_to_all(
        jnp.take(retained, first_index, axis=0, mode="clip"), "req", 0, 0, tiled=True
    )
    for bits, index in zip(partner_bits, pair_index):
        pairs = [(i, i ^ bits) for i in range(owners)]
        if bits == 1:
            outgoing = jnp.take(retained, index, axis=0, mode="clip")
            state_pieces.append(lax.ppermute(outgoing, "req", pairs))
            continue
        arrived = lax.dynamic_slice_in_dim(
            first_arrivals, (req_index ^ bits) * first_slots, first_slots, 0
        )
        buffer = jnp.concatenate(
            [arrived, jnp.zeros((cap - first_slots,) + arrived.shape[1:], arrived.dtype)], axis=0
        )
        needed = jnp.max(pair_count[owner_ids, owner_ids ^ bits])
        needed = jnp.clip(lax.pmax(needed, "group"), first_slots, cap)

        def one_slot(slot, held, index=index, pairs=pairs):
            row = lax.dynamic_index_in_dim(retained, index[slot], 0, keepdims=True)
            got = lax.ppermute(row, "req", pairs)
            return lax.dynamic_update_index_in_dim(held, got, slot, 0)

        state_pieces.append(lax.fori_loop(first_slots, needed, one_slot, buffer))
    piece_of = jnp.clip(arriving_source ^ req_index, 0, owners - 1)
    slot_of = jnp.clip(arriving_rank, 0, cap - 1)

    def place(row, held):
        slot = slot_of[row]
        chosen = lax.dynamic_index_in_dim(state_pieces[0], slot, 0, keepdims=True)
        for which in range(1, len(state_pieces)):
            candidate = lax.dynamic_index_in_dim(state_pieces[which], slot, 0, keepdims=True)
            chosen = jnp.where(piece_of[row] == which, candidate, chosen)
        return lax.dynamic_update_index_in_dim(held, chosen, row, 0)

    new_ssm_state = lax.fori_loop(
        0, local_requests, place, jnp.zeros_like(retained)
    )
    new_conv_x_state = hand_over(kept_x)
    new_conv_bc_state = hand_over(kept_bc)
    return (mixed, new_ssm_state, new_conv_x_state, new_conv_bc_state)


def solution(mesh):
    placed = (
        P(("group", "req"), None, "head"),
        P(("group", "req"), None, "head"),
        P(("group", "req"), None, None),
        P(("group", "req"), None, "head"),
        P(("group", "req"), None, "head"),
        P(("group", "req"), None, None),
        P(("group", "req"), "head", None, None),
        P(("group", "req")),
        P("group"),
        P(None, "head"),
        P("head"),
        P(),
        P(),
        P("head"),
        P("head"),
        P("head"),
        P("head"),
        P("head", None),
    )
    return jax.shard_map(
        on_device,
        mesh=mesh,
        in_specs=placed,
        out_specs=(
            P(("group", "req"), None, "head"),
            P(("group", "req"), "head", None, None),
            P(("group", "req"), None, "head"),
            P(("group", "req"), None, None),
        ),
        check_vma=False,
    )
```

```python
import jax
import jax.numpy as jnp
from jax import lax
from jax.sharding import PartitionSpec as P

D = 8192
H = 256
P_SIZE = 64
N = 256
G = 8
K = 4
L = 8
CAP = 8


epsilon = 1e-05
highest = lax.Precision.HIGH


def conv_window(history, inputs, weight, bias_vector):
    joined = jnp.concatenate([history, inputs], axis=1)
    widened = joined.astype(jnp.float32)
    accumulated = bias_vector[None, None, :] + weight[0][None, None, :] * widened[:, 0:L, :]
    for offset in range(1, K):
        accumulated = (
            accumulated + weight[offset][None, None, :] * widened[:, offset : offset + L, :]
        )
    return (jax.nn.silu(accumulated), joined)


def on_device(
    x_input,
    z_input,
    bc_input,
    dt_input,
    conv_x_state,
    conv_bc_state,
    ssm_state,
    accepted,
    next_owner,
    conv_x_weight,
    conv_x_bias,
    conv_bc_weight,
    conv_bc_bias,
    dt_bias,
    a_log,
    d_skip,
    norm_gain,
    out_weight,
):
    local_requests = x_input.shape[0]
    local_heads = dt_input.shape[2]
    head_index = lax.axis_index("head")
    req_index = lax.axis_index("req")
    all_requests = next_owner.shape[0]
    heads_group = H // G
    x_conv, x_joined = conv_window(conv_x_state, x_input, conv_x_weight, conv_x_bias)
    bc_conv, bc_joined = conv_window(conv_bc_state, bc_input, conv_bc_weight, conv_bc_bias)
    step_size = jax.nn.softplus(dt_input + dt_bias[None, None, :])
    log_decay = -jnp.exp(a_log)[None, None, :] * step_size
    global_heads = head_index * local_heads + jnp.arange(local_heads, dtype=jnp.int32)
    group_pick = (
        global_heads[:, None] // heads_group == jnp.arange(G, dtype=jnp.int32)[None, :]
    ).astype(jnp.float32)
    b_groups = bc_conv[:, :, : G * N].reshape(local_requests, L, G, N)
    c_groups = bc_conv[:, :, G * N :].reshape(local_requests, L, G, N)
    b_heads = jnp.einsum("rlgn,hg->rlhn", b_groups, group_pick, precision=highest)
    c_heads = jnp.einsum("rlgn,hg->rlhn", c_groups, group_pick, precision=highest)
    x_heads = x_conv.reshape(local_requests, L, local_heads, P_SIZE)
    initial = ssm_state.astype(jnp.float32)
    inclusive = jnp.cumsum(log_decay, axis=1)
    before = jnp.concatenate(
        [jnp.zeros((local_requests, 1, local_heads), jnp.float32), inclusive], axis=1
    )
    positions = jnp.arange(L, dtype=jnp.int32)
    causal = positions[:, None] >= positions[None, :]
    by_head = inclusive.transpose(0, 2, 1)
    differences = by_head[:, :, :, None] - by_head[:, :, None, :]
    pair_decay = jnp.exp(jnp.where(causal[None, None], differences, -jnp.inf))
    scores = jnp.einsum("rthn,rshn->rhts", c_heads, b_heads, precision=highest)
    weights = scores * pair_decay * step_size.transpose(0, 2, 1)[:, :, None, :]
    within = jnp.einsum("rhts,rshp->rthp", weights, x_heads, precision=highest)
    carried = jnp.exp(inclusive)[:, :, :, None] * jnp.einsum(
        "rhpn,rthn->rthp", initial, c_heads, precision=highest
    )
    y_values = within + carried + d_skip[None, None, :, None] * x_heads
    count_pick = (jnp.arange(L + 1, dtype=jnp.int32)[None, :] == accepted[:, None]).astype(
        jnp.float32
    )
    reached = jnp.einsum("ra,rah->rh", count_pick, before, precision=highest)
    valid = positions[None, :] < accepted[:, None]
    exponent = jnp.where(valid[:, :, None], reached[:, None, :] - inclusive, -jnp.inf)
    token_weight = jnp.exp(exponent) * step_size
    weighted_x = token_weight[:, :, :, None] * x_heads
    retained = jnp.exp(reached)[:, :, None, None] * initial + jnp.einsum(
        "rshp,rshn->rhpn", weighted_x, b_heads, precision=highest
    )
    retained = retained.astype(jnp.bfloat16)
    gated = y_values.reshape(local_requests, L, local_heads * P_SIZE) * jax.nn.silu(
        z_input.astype(jnp.float32)
    )
    blocks = gated.reshape(local_requests, L, local_heads, P_SIZE)
    inverse_rms = lax.rsqrt(jnp.mean(blocks * blocks, axis=3, keepdims=True) + epsilon)
    normed = (
        (blocks * inverse_rms).reshape(local_requests, L, local_heads * P_SIZE)
        * norm_gain[None, None, :]
    ).astype(jnp.bfloat16)
    partial_terms = jnp.dot(
        normed.reshape(local_requests * L, local_heads * P_SIZE),
        out_weight,
        preferred_element_type=jnp.float32,
    )
    share_width = D // lax.axis_size("head")
    share = lax.psum_scatter(partial_terms, "head", scatter_dimension=1, tiled=True)
    mixed = share.astype(jnp.bfloat16).reshape(local_requests, L, share_width)
    window_rows = jnp.arange(K - 1 + L, dtype=jnp.int32)
    row_pick = (
        window_rows[None, None, :]
        == accepted[:, None, None] + jnp.arange(K - 1, dtype=jnp.int32)[None, :, None]
    ).astype(jnp.bfloat16)
    kept_x = jnp.einsum(
        "rkt,rtc->rkc", row_pick, x_joined, preferred_element_type=jnp.float32
    ).astype(jnp.bfloat16)
    kept_bc = jnp.einsum(
        "rkt,rtc->rkc", row_pick, bc_joined, preferred_element_type=jnp.float32
    ).astype(jnp.bfloat16)
    requests_per_owner = local_requests
    owners = lax.axis_size("req")
    cap = min(CAP, local_requests)
    request_ids = jnp.arange(all_requests, dtype=jnp.int32)
    source = request_ids // requests_per_owner
    same_owner = next_owner[:, None] == next_owner[None, :]
    earlier = request_ids[None, :] < request_ids[:, None]
    rank_at_owner = jnp.sum((same_owner & earlier).astype(jnp.int32), axis=1)
    same_source = source[:, None] == source[None, :]
    rank_in_pair = jnp.sum((same_owner & earlier & same_source).astype(jnp.int32), axis=1)
    local_owner = lax.dynamic_slice_in_dim(next_owner, req_index * local_requests, local_requests)
    local_rank = lax.dynamic_slice_in_dim(rank_in_pair, req_index * local_requests, local_requests)
    slot_rows = jnp.arange(local_requests, dtype=jnp.int32)
    chosen = (local_owner[None, None, :] == jnp.arange(owners, dtype=jnp.int32)[:, None, None]) & (
        local_rank[None, None, :] == jnp.arange(cap, dtype=jnp.int32)[None, :, None]
    )
    send_index = jnp.sum(jnp.where(chosen, slot_rows[None, None, :], 0), axis=2).reshape(-1)
    arriving = (next_owner[None, :] == req_index) & (rank_at_owner[None, :] == slot_rows[:, None])
    receive_index = jnp.sum(
        jnp.where(arriving, source[None, :] * cap + rank_in_pair[None, :], 0), axis=1
    )

    partner_bits = range(1, owners)
    own_index = jnp.take(send_index.reshape(owners, cap), req_index, axis=0)
    pair_index = [
        jnp.take(send_index.reshape(owners, cap), req_index ^ bits, axis=0) for bits in partner_bits
    ]
    arriving_source = jnp.sum(jnp.where(arriving, source[None, :], 0), axis=1)
    arriving_rank = jnp.sum(jnp.where(arriving, rank_in_pair[None, :], 0), axis=1)
    gather_index = (arriving_source ^ req_index) * cap + arriving_rank

    def send_pieces(values):
        pieces = [jnp.take(values, own_index, axis=0, mode="clip")]
        for bits, index in zip(partner_bits, pair_index):
            outgoing = jnp.take(values, index, axis=0, mode="clip")
            pairs = [(i, i ^ bits) for i in range(owners)]
            pieces.append(lax.ppermute(outgoing, "req", pairs))
        return pieces

    def hand_over(values):
        pieces = send_pieces(values)
        return jnp.take(jnp.concatenate(pieces, axis=0), gather_index, axis=0, mode="clip")

    owner_ids = jnp.arange(owners, dtype=jnp.int32)
    pair_count = jnp.sum(
        (
            (source[None, None, :] == owner_ids[:, None, None])
            & (next_owner[None, None, :] == owner_ids[None, :, None])
        ).astype(jnp.int32),
        axis=2,
    )
    first_slots = min(3, cap)
    state_pieces = [jnp.take(retained, own_index, axis=0, mode="clip")]
    first_index = send_index.reshape(owners, cap)[:, :first_slots].reshape(-1)
    first_arrivals = lax.all_to_all(
        jnp.take(retained, first_index, axis=0, mode="clip"), "req", 0, 0, tiled=True
    )
    for bits, index in zip(partner_bits, pair_index):
        pairs = [(i, i ^ bits) for i in range(owners)]
        if bits == 1:
            outgoing = jnp.take(retained, index, axis=0, mode="clip")
            state_pieces.append(lax.ppermute(outgoing, "req", pairs))
            continue
        arrived = lax.dynamic_slice_in_dim(
            first_arrivals, (req_index ^ bits) * first_slots, first_slots, 0
        )
        buffer = jnp.concatenate(
            [arrived, jnp.zeros((cap - first_slots,) + arrived.shape[1:], arrived.dtype)], axis=0
        )
        needed = jnp.max(pair_count[owner_ids, owner_ids ^ bits])
        needed = jnp.clip(lax.pmax(needed, "group"), first_slots, cap)

        def one_slot(slot, held, index=index, pairs=pairs):
            row = lax.dynamic_index_in_dim(retained, index[slot], 0, keepdims=True)
            got = lax.ppermute(row, "req", pairs)
            return lax.dynamic_update_index_in_dim(held, got, slot, 0)

        state_pieces.append(lax.fori_loop(first_slots, needed, one_slot, buffer))
    piece_of = jnp.clip(arriving_source ^ req_index, 0, owners - 1)
    slot_of = jnp.clip(arriving_rank, 0, cap - 1)

    def place(row, held):
        slot = slot_of[row]
        chosen = lax.dynamic_index_in_dim(state_pieces[0], slot, 0, keepdims=True)
        for which in range(1, len(state_pieces)):
            candidate = lax.dynamic_index_in_dim(state_pieces[which], slot, 0, keepdims=True)
            chosen = jnp.where(piece_of[row] == which, candidate, chosen)
        return lax.dynamic_update_index_in_dim(held, chosen, row, 0)

    new_ssm_state = jnp.zeros_like(retained)
    for row in range(local_requests):
        new_ssm_state = place(row, new_ssm_state)
    new_conv_x_state = hand_over(kept_x)
    new_conv_bc_state = hand_over(kept_bc)
    return (mixed, new_ssm_state, new_conv_x_state, new_conv_bc_state)


def solution(mesh):
    placed = (
        P(("group", "req"), None, "head"),
        P(("group", "req"), None, "head"),
        P(("group", "req"), None, None),
        P(("group", "req"), None, "head"),
        P(("group", "req"), None, "head"),
        P(("group", "req"), None, None),
        P(("group", "req"), "head", None, None),
        P(("group", "req")),
        P("group"),
        P(None, "head"),
        P("head"),
        P(),
        P(),
        P("head"),
        P("head"),
        P("head"),
        P("head"),
        P("head", None),
    )
    return jax.shard_map(
        on_device,
        mesh=mesh,
        in_specs=placed,
        out_specs=(
            P(("group", "req"), None, "head"),
            P(("group", "req"), "head", None, None),
            P(("group", "req"), None, "head"),
            P(("group", "req"), None, None),
        ),
        check_vma=False,
    )
```

```python
import jax
import jax.numpy as jnp
from jax import lax
from jax.sharding import PartitionSpec as P

D = 8192
H = 256
P_SIZE = 64
N = 256
G = 8
K = 4
L = 8
CAP = 8


epsilon = 1e-05
highest = lax.Precision.HIGH


def conv_window(history, inputs, weight, bias_vector):
    joined = jnp.concatenate([history, inputs], axis=1)
    widened = joined.astype(jnp.float32)
    accumulated = bias_vector[None, None, :] + weight[0][None, None, :] * widened[:, 0:L, :]
    for offset in range(1, K):
        accumulated = (
            accumulated + weight[offset][None, None, :] * widened[:, offset : offset + L, :]
        )
    return (jax.nn.silu(accumulated), joined)


def on_device(
    x_input,
    z_input,
    bc_input,
    dt_input,
    conv_x_state,
    conv_bc_state,
    ssm_state,
    accepted,
    next_owner,
    conv_x_weight,
    conv_x_bias,
    conv_bc_weight,
    conv_bc_bias,
    dt_bias,
    a_log,
    d_skip,
    norm_gain,
    out_weight,
):
    local_requests = x_input.shape[0]
    local_heads = dt_input.shape[2]
    head_index = lax.axis_index("head")
    req_index = lax.axis_index("req")
    all_requests = next_owner.shape[0]
    heads_group = H // G
    x_conv, x_joined = conv_window(conv_x_state, x_input, conv_x_weight, conv_x_bias)
    bc_conv, bc_joined = conv_window(conv_bc_state, bc_input, conv_bc_weight, conv_bc_bias)
    step_size = jax.nn.softplus(dt_input + dt_bias[None, None, :])
    log_decay = -jnp.exp(a_log)[None, None, :] * step_size
    global_heads = head_index * local_heads + jnp.arange(local_heads, dtype=jnp.int32)
    group_pick = (
        global_heads[:, None] // heads_group == jnp.arange(G, dtype=jnp.int32)[None, :]
    ).astype(jnp.float32)
    b_groups = bc_conv[:, :, : G * N].reshape(local_requests, L, G, N)
    c_groups = bc_conv[:, :, G * N :].reshape(local_requests, L, G, N)
    b_heads = jnp.einsum("rlgn,hg->rlhn", b_groups, group_pick, precision=highest)
    c_heads = jnp.einsum("rlgn,hg->rlhn", c_groups, group_pick, precision=highest)
    x_heads = x_conv.reshape(local_requests, L, local_heads, P_SIZE)
    initial = ssm_state.astype(jnp.float32)
    inclusive = jnp.cumsum(log_decay, axis=1)
    before = jnp.concatenate(
        [jnp.zeros((local_requests, 1, local_heads), jnp.float32), inclusive], axis=1
    )
    positions = jnp.arange(L, dtype=jnp.int32)
    causal = positions[:, None] >= positions[None, :]
    by_head = inclusive.transpose(0, 2, 1)
    differences = by_head[:, :, :, None] - by_head[:, :, None, :]
    pair_decay = jnp.exp(jnp.where(causal[None, None], differences, -jnp.inf))
    scores = jnp.einsum("rthn,rshn->rhts", c_heads, b_heads, precision=highest)
    weights = scores * pair_decay * step_size.transpose(0, 2, 1)[:, :, None, :]
    within = jnp.einsum("rhts,rshp->rthp", weights, x_heads, precision=highest)
    carried = jnp.exp(inclusive)[:, :, :, None] * jnp.einsum(
        "rhpn,rthn->rthp", initial, c_heads, precision=highest
    )
    y_values = within + carried + d_skip[None, None, :, None] * x_heads
    count_pick = (jnp.arange(L + 1, dtype=jnp.int32)[None, :] == accepted[:, None]).astype(
        jnp.float32
    )
    reached = jnp.einsum("ra,rah->rh", count_pick, before, precision=highest)
    valid = positions[None, :] < accepted[:, None]
    exponent = jnp.where(valid[:, :, None], reached[:, None, :] - inclusive, -jnp.inf)
    token_weight = jnp.exp(exponent) * step_size
    weighted_x = token_weight[:, :, :, None] * x_heads
    retained = jnp.exp(reached)[:, :, None, None] * initial + jnp.einsum(
        "rshp,rshn->rhpn", weighted_x, b_heads, precision=highest
    )
    retained = retained.astype(jnp.bfloat16)
    gated = y_values.reshape(local_requests, L, local_heads * P_SIZE) * jax.nn.silu(
        z_input.astype(jnp.float32)
    )
    blocks = gated.reshape(local_requests, L, local_heads, P_SIZE)
    inverse_rms = lax.rsqrt(jnp.mean(blocks * blocks, axis=3, keepdims=True) + epsilon)
    normed = (
        (blocks * inverse_rms).reshape(local_requests, L, local_heads * P_SIZE)
        * norm_gain[None, None, :]
    ).astype(jnp.bfloat16)
    partial_terms = jnp.dot(
        normed.reshape(local_requests * L, local_heads * P_SIZE),
        out_weight,
        preferred_element_type=jnp.float32,
    )
    share_width = D // lax.axis_size("head")
    share = lax.psum_scatter(partial_terms, "head", scatter_dimension=1, tiled=True)
    mixed = share.astype(jnp.bfloat16).reshape(local_requests, L, share_width)
    window_rows = jnp.arange(K - 1 + L, dtype=jnp.int32)
    row_pick = (
        window_rows[None, None, :]
        == accepted[:, None, None] + jnp.arange(K - 1, dtype=jnp.int32)[None, :, None]
    ).astype(jnp.bfloat16)
    kept_x = jnp.einsum(
        "rkt,rtc->rkc", row_pick, x_joined, preferred_element_type=jnp.float32
    ).astype(jnp.bfloat16)
    kept_bc = jnp.einsum(
        "rkt,rtc->rkc", row_pick, bc_joined, preferred_element_type=jnp.float32
    ).astype(jnp.bfloat16)
    requests_per_owner = local_requests
    owners = lax.axis_size("req")
    cap = min(CAP, local_requests)
    request_ids = jnp.arange(all_requests, dtype=jnp.int32)
    source = request_ids // requests_per_owner
    same_owner = next_owner[:, None] == next_owner[None, :]
    earlier = request_ids[None, :] < request_ids[:, None]
    rank_at_owner = jnp.sum((same_owner & earlier).astype(jnp.int32), axis=1)
    same_source = source[:, None] == source[None, :]
    rank_in_pair = jnp.sum((same_owner & earlier & same_source).astype(jnp.int32), axis=1)
    local_owner = lax.dynamic_slice_in_dim(next_owner, req_index * local_requests, local_requests)
    local_rank = lax.dynamic_slice_in_dim(rank_in_pair, req_index * local_requests, local_requests)
    slot_rows = jnp.arange(local_requests, dtype=jnp.int32)
    chosen = (local_owner[None, None, :] == jnp.arange(owners, dtype=jnp.int32)[:, None, None]) & (
        local_rank[None, None, :] == jnp.arange(cap, dtype=jnp.int32)[None, :, None]
    )
    send_index = jnp.sum(jnp.where(chosen, slot_rows[None, None, :], 0), axis=2).reshape(-1)
    arriving = (next_owner[None, :] == req_index) & (rank_at_owner[None, :] == slot_rows[:, None])
    receive_index = jnp.sum(
        jnp.where(arriving, source[None, :] * cap + rank_in_pair[None, :], 0), axis=1
    )

    partner_bits = range(1, owners)
    own_index = jnp.take(send_index.reshape(owners, cap), req_index, axis=0)
    pair_index = [
        jnp.take(send_index.reshape(owners, cap), req_index ^ bits, axis=0) for bits in partner_bits
    ]
    arriving_source = jnp.sum(jnp.where(arriving, source[None, :], 0), axis=1)
    arriving_rank = jnp.sum(jnp.where(arriving, rank_in_pair[None, :], 0), axis=1)
    gather_index = (arriving_source ^ req_index) * cap + arriving_rank

    def send_pieces(values):
        pieces = [jnp.take(values, own_index, axis=0, mode="clip")]
        for bits, index in zip(partner_bits, pair_index):
            outgoing = jnp.take(values, index, axis=0, mode="clip")
            pairs = [(i, i ^ bits) for i in range(owners)]
            pieces.append(lax.ppermute(outgoing, "req", pairs))
        return pieces

    def hand_over(values):
        pieces = send_pieces(values)
        return jnp.take(jnp.concatenate(pieces, axis=0), gather_index, axis=0, mode="clip")

    owner_ids = jnp.arange(owners, dtype=jnp.int32)
    pair_count = jnp.sum(
        (
            (source[None, None, :] == owner_ids[:, None, None])
            & (next_owner[None, None, :] == owner_ids[None, :, None])
        ).astype(jnp.int32),
        axis=2,
    )
    first_slots = min(3, cap)
    state_pieces = [jnp.take(retained, own_index, axis=0, mode="clip")]
    first_index = send_index.reshape(owners, cap)[:, :first_slots].reshape(-1)
    first_outgoing = jnp.concatenate(
        [
            lax.dynamic_index_in_dim(retained, first_index[i], 0, keepdims=True)
            for i in range(first_index.shape[0])
        ],
        axis=0,
    )
    first_arrivals = lax.all_to_all(first_outgoing, "req", 0, 0, tiled=True)
    for bits, index in zip(partner_bits, pair_index):
        pairs = [(i, i ^ bits) for i in range(owners)]
        if bits == 1:
            outgoing = jnp.take(retained, index, axis=0, mode="clip")
            state_pieces.append(lax.ppermute(outgoing, "req", pairs))
            continue
        arrived = lax.dynamic_slice_in_dim(
            first_arrivals, (req_index ^ bits) * first_slots, first_slots, 0
        )
        buffer = jnp.concatenate(
            [arrived, jnp.zeros((cap - first_slots,) + arrived.shape[1:], arrived.dtype)], axis=0
        )
        needed = jnp.max(pair_count[owner_ids, owner_ids ^ bits])
        needed = jnp.clip(lax.pmax(needed, "group"), first_slots, cap)

        def one_slot(slot, held, index=index, pairs=pairs):
            row = lax.dynamic_index_in_dim(retained, index[slot], 0, keepdims=True)
            got = lax.ppermute(row, "req", pairs)
            return lax.dynamic_update_index_in_dim(held, got, slot, 0)

        state_pieces.append(lax.fori_loop(first_slots, needed, one_slot, buffer))
    piece_of = jnp.clip(arriving_source ^ req_index, 0, owners - 1)
    slot_of = jnp.clip(arriving_rank, 0, cap - 1)

    def place(row, held):
        slot = slot_of[row]
        chosen = lax.dynamic_index_in_dim(state_pieces[0], slot, 0, keepdims=True)
        for which in range(1, len(state_pieces)):
            candidate = lax.dynamic_index_in_dim(state_pieces[which], slot, 0, keepdims=True)
            chosen = jnp.where(piece_of[row] == which, candidate, chosen)
        return lax.dynamic_update_index_in_dim(held, chosen, row, 0)

    new_ssm_state = jnp.zeros_like(retained)
    for row in range(local_requests):
        new_ssm_state = place(row, new_ssm_state)
    new_conv_x_state = hand_over(kept_x)
    new_conv_bc_state = hand_over(kept_bc)
    return (mixed, new_ssm_state, new_conv_x_state, new_conv_bc_state)


def solution(mesh):
    placed = (
        P(("group", "req"), None, "head"),
        P(("group", "req"), None, "head"),
        P(("group", "req"), None, None),
        P(("group", "req"), None, "head"),
        P(("group", "req"), None, "head"),
        P(("group", "req"), None, None),
        P(("group", "req"), "head", None, None),
        P(("group", "req")),
        P("group"),
        P(None, "head"),
        P("head"),
        P(),
        P(),
        P("head"),
        P("head"),
        P("head"),
        P("head"),
        P("head", None),
    )
    return jax.shard_map(
        on_device,
        mesh=mesh,
        in_specs=placed,
        out_specs=(
            P(("group", "req"), None, "head"),
            P(("group", "req"), "head", None, None),
            P(("group", "req"), None, "head"),
            P(("group", "req"), None, None),
        ),
        check_vma=False,
    )
```
